256 devices in a mesh: seq: 16 (over y_lo, z), head: 16 (over y_hi, x, core).
Axes of the slice: x: 4, y: 4 (y_hi: 2, y_lo: 2; y = y_hi * 2 + y_lo), z: 8, core: 2. Of those that a mesh axis runs over, the one named last changes fastest.
Arguments:
- queries: bfloat16 [16384, 4096], P('seq', 'head'), may hold values from -7 to 7
- key_tokens: bfloat16 [16384, 4096], P('seq', 'head'), may hold values from -7 to 7
- value_tokens: bfloat16 [16384, 4096], P('seq', 'head'), may hold values from -7 to 7
- pattern: int32 [256, 32], P('seq'), may hold values from 0 to 255, as said below
- w_out: bfloat16 [4096, 5120], P('head'), may hold values from -0.1875 to 0.1875
- out_gate: float32 [5120], replicated, may hold values from 0.25 to 1.75
Outputs:
- block_out: bfloat16 [16384, 5120], P(('seq', 'head'))
The draws below stay inside these ranges and needn't reach their ends.
Inputs may be any that keep to these rules, and one draw needn't show every extreme that they name: `pattern`: row c lists 32 distinct key cubes, c itself among them. For every two different indices a and b of seq, the cubes held by b that are listed in the rows of the cubes held by a are exactly 6 distinct cubes.
All inputs are finite; a program needn't handle non-finite values.
Results may differ from the reference program's by a relative error of at most 0.014.
Values may be sent and summed in bfloat16 or wider, within the bound.
No kernel may reach another device: no remote copies, remote signals or barrier semaphores. Data moves between devices by JAX's collectives and lax.ppermute only.
A program may use at most 128 MiB of HBM per device.

```python
import math
import jax
import jax.numpy as jnp
from jax import lax

D = 5120
HEAD_DIM = 128
HEAD_DEV = 2
CUBE = 64
CUBES_DEV = 16
HEADS = 32
CUBES = 256
TOKENS = 16384
SEL = 32
CAP = 6
N_SEQ = 16


def cube_field(key, first, second):
    shared_key = jax.random.fold_in(key, first)
    noise_key = jax.random.fold_in(key, second)
    shared = jax.random.normal(shared_key, (CUBES, HEADS, HEAD_DIM), jnp.float32)
    noise_draw = 0.7 * jax.random.normal(noise_key, (TOKENS, HEADS, HEAD_DIM), jnp.float32)
    return jnp.repeat(shared, CUBE, axis=0) + noise_draw


def draw_queries(key, part):
    drawn = 1.4 * jax.random.normal(key, (TOKENS, HEADS, HEAD_DIM), jnp.float32)
    drawn = jnp.clip(drawn, -7.0, 7.0)
    return drawn.reshape(TOKENS, HEADS * HEAD_DIM).astype(jnp.bfloat16)


def draw_key_tokens(key, part):
    drawn = cube_field(key, 17, 18)
    drawn = jnp.clip(drawn, -7.0, 7.0)
    return drawn.reshape(TOKENS, HEADS * HEAD_DIM).astype(jnp.bfloat16)


def draw_value_tokens(key, part):
    drawn = jnp.clip(cube_field(key, 27, 28), -7.0, 7.0)
    return drawn.reshape(TOKENS, HEADS * HEAD_DIM).astype(jnp.bfloat16)


def draw_pattern(key, part):
    remote = (N_SEQ - 1) * CAP
    forced = (remote + CUBES_DEV - 1) // CUBES_DEV
    cand_total = remote + CUBES_DEV - 1
    pick_keys = jax.random.split(jax.random.fold_in(key, 41), N_SEQ * (N_SEQ - 1))
    picked = jax.vmap(lambda sub_key: jax.random.permutation(sub_key, CUBES_DEV)[:CAP])(pick_keys)
    picked = picked.reshape(N_SEQ, N_SEQ - 1, CAP).astype(jnp.int32)
    device = jnp.arange(N_SEQ, dtype=jnp.int32)[:, None, None]
    cube_no = jnp.arange(CUBES_DEV, dtype=jnp.int32)[None, :, None]
    cand_no = jnp.arange(cand_total, dtype=jnp.int32)[None, None, :]
    is_forced = (cand_no >= forced * cube_no) & (cand_no < forced * cube_no + forced) & (cand_no < remote)
    noise_draw = jax.random.randint(jax.random.fold_in(key, 42), (N_SEQ, CUBES_DEV, cand_total), 0, 2 ** 18)
    ranking = jnp.where(is_forced, cand_no, 4096 + noise_draw * 4096 + cand_no)
    picked_ids = jnp.argsort(ranking, axis=-1)[:, :, :SEL - 1].astype(jnp.int32)
    other_dev = jnp.minimum(picked_ids // CAP, N_SEQ - 2)
    slot_no = picked_ids % CAP
    source = other_dev + (other_dev >= device).astype(jnp.int32)
    dev_grid = jnp.broadcast_to(device, picked_ids.shape)
    remote_cube = source * CUBES_DEV + picked[dev_grid, other_dev, slot_no]
    own_no = picked_ids - remote
    own_local = own_no + (own_no >= cube_no).astype(jnp.int32)
    own_cube = device * CUBES_DEV + own_local
    listed = jnp.where(picked_ids < remote, remote_cube, own_cube)
    self_cube = jnp.broadcast_to(device * CUBES_DEV + cube_no, (N_SEQ, CUBES_DEV, 1))
    listed = jnp.concatenate([self_cube, listed], axis=-1).astype(jnp.int32)
    shuffle = jax.random.randint(jax.random.fold_in(key, 43), listed.shape, 0, 2 ** 18) * 4096 + jnp.arange(SEL, dtype=jnp.int32)
    listed = jnp.take_along_axis(listed, jnp.argsort(shuffle, axis=-1), axis=-1)
    return listed.reshape(CUBES, SEL).astype(jnp.int32)


def shard_levels(key, extent, cuts, low, top_value):
    loudness = 1.0
    for dim, shards_of in cuts:
        heights = jax.random.uniform(jax.random.fold_in(jax.random.fold_in(key, 6), dim), (shards_of,), jnp.float32, low / len(cuts), top_value / len(cuts))
        loudness = loudness * jnp.repeat(jnp.exp(heights), extent[dim] // shards_of).reshape((-1,) + (1,) * (len(extent) - 1 - dim))
    return loudness


def scatter_about(own_key, dims, spread, bound, shards=(), kind=jnp.bfloat16):
    array = jax.random.normal(own_key, dims, jnp.float32) * spread
    if len(shards) > 0:
        array = shard_levels(own_key, dims, shards, -0.22, 0.18) * array
    return jnp.clip(array, min=-bound, max=bound).astype(kind)


def setup_inputs(seed: int = 0) -> dict:
    streams_of = jax.random.split(jax.random.key(seed), 7)
    return {
        "queries": draw_queries(jax.random.fold_in(streams_of[6], 71), 0),
        "key_tokens": draw_key_tokens(jax.random.fold_in(streams_of[6], 71), 0),
        "value_tokens": draw_value_tokens(jax.random.fold_in(streams_of[6], 71), 0),
        "pattern": draw_pattern(jax.random.fold_in(streams_of[6], 71), 0),
        "w_out": scatter_about(streams_of[4], (HEADS * HEAD_DIM, D), (8 * HEAD_DIM) ** -0.5, 0.1875, ((0, 16),)),
        "out_gate": jnp.clip(1.0 + 0.15 * jax.random.normal(streams_of[5], (D,), jnp.float32), 0.25, 1.75),
    }


def softmax_rounded(scores):
    largest = jnp.max(scores, axis=-1, keepdims=True)
    raised = jnp.exp(scores - largest)
    weights = raised / jnp.sum(raised, axis=-1, keepdims=True)
    return lax.optimization_barrier(weights.astype(jnp.bfloat16)).astype(jnp.float32)


def reference(queries, key_tokens, value_tokens, pattern, w_out, out_gate):
    feat_width = HEADS * HEAD_DIM
    score_scale = HEAD_DIM ** -0.5
    q_heads = queries.astype(jnp.float32).reshape(CUBES, CUBE, HEADS, HEAD_DIM)
    k_heads = key_tokens.astype(jnp.float32).reshape(CUBES, CUBE, HEADS, HEAD_DIM)
    v_heads = value_tokens.astype(jnp.float32).reshape(CUBES, CUBE, HEADS, HEAD_DIM)
    pooled_k = jnp.mean(k_heads, axis=1).astype(jnp.bfloat16)
    pooled_v = jnp.mean(v_heads, axis=1).astype(jnp.bfloat16)
    pooled_k32 = lax.optimization_barrier(pooled_k).astype(jnp.float32)
    pooled_v32 = lax.optimization_barrier(pooled_v).astype(jnp.float32)
    per_block = math.gcd(CUBES, max(1, 512 // CUBE))
    blocks = CUBES // per_block

    def one_block(inputs):
        q_block, row_ids = inputs
        sel_k = k_heads[row_ids].reshape(per_block, SEL * CUBE, HEADS, HEAD_DIM)
        sel_v = v_heads[row_ids].reshape(per_block, SEL * CUBE, HEADS, HEAD_DIM)
        fine_w = softmax_rounded(jnp.einsum("gqhd,gkhd->ghqk", q_block, sel_k) * score_scale)
        fine_out = jnp.einsum("ghqk,gkhd->gqhd", fine_w, sel_v)
        coarse_w = softmax_rounded(jnp.einsum("gqhd,chd->ghqc", q_block, pooled_k32) * score_scale)
        coarse_out = jnp.einsum("ghqc,chd->gqhd", coarse_w, pooled_v32)
        return (fine_out + coarse_out).astype(jnp.bfloat16)

    attended = lax.map(one_block, (q_heads.reshape(blocks, per_block, CUBE, HEADS, HEAD_DIM), pattern.reshape(blocks, per_block, SEL)))
    attended = attended.reshape(TOKENS, feat_width)
    group_width = HEAD_DEV * HEAD_DIM

    def add_group(running, number):
        columns = lax.dynamic_slice_in_dim(attended, number * group_width, group_width, 1)
        weight_rows = lax.dynamic_slice_in_dim(w_out, number * group_width, group_width, 0)
        term = jnp.dot(columns, weight_rows, preferred_element_type=jnp.float32).astype(jnp.bfloat16)
        return running + lax.optimization_barrier(term).astype(jnp.float32), None

    projected, _ = lax.scan(add_group, jnp.zeros((TOKENS, D), jnp.float32), jnp.arange(HEADS // HEAD_DEV, dtype=jnp.int32))
    return (projected * out_gate[None, :]).astype(jnp.bfloat16)
```

```python
import functools

import jax
import jax.numpy as jnp
from jax import lax
from jax.experimental import pallas as pl
from jax.experimental.pallas import tpu as pltpu
from jax.sharding import PartitionSpec as P

HEAD_DIM = 128
CUBE = 64
CAP = 6


def attend_kernel(tbl_ref, q_ref, ok_ref, ov_ref, rv_ref, pk_ref, pv_ref, o_ref, kbuf, vbuf,
                  *, n_sel, cubes_here, heads_here):
    i = pl.program_id(0)
    scale = HEAD_DIM ** (-0.5)

    def fill(j, carry):
        s = tbl_ref[i, j]
        dst = pl.ds(pl.multiple_of(j * CUBE, CUBE), CUBE)

        @pl.when(s < cubes_here)
        def _():
            kbuf[dst, :] = ok_ref[s]
            vbuf[dst, :] = ov_ref[s]

        @pl.when(s >= cubes_here)
        def _():
            t = s - cubes_here
            a = t // CAP
            base = pl.multiple_of((t % CAP) * (2 * CUBE), 2 * CUBE)
            kbuf[dst, :] = rv_ref[a, pl.ds(base, CUBE), :]
            vbuf[dst, :] = rv_ref[a, pl.ds(base + CUBE, CUBE), :]

        return carry

    lax.fori_loop(0, n_sel, fill, 0)

    def softmax_w(s):
        m = jnp.max(s, axis=-1, keepdims=True)
        p = jnp.exp(s - m)
        return (p / jnp.sum(p, axis=-1, keepdims=True)).astype(jnp.bfloat16)

    dims = (((1,), (1,)), ((), ()))
    for h in range(heads_here):
        cols = slice(h * HEAD_DIM, (h + 1) * HEAD_DIM)
        q = q_ref[:, cols]
        s_f = lax.dot_general(q, kbuf[:, cols], dims, preferred_element_type=jnp.float32) * scale
        fine = jnp.dot(softmax_w(s_f), vbuf[:, cols], preferred_element_type=jnp.float32)
        s_c = lax.dot_general(q, pk_ref[:, cols], dims, preferred_element_type=jnp.float32) * scale
        coarse = jnp.dot(softmax_w(s_c), pv_ref[:, cols], preferred_element_type=jnp.float32)
        o_ref[:, cols] = (fine + coarse).astype(jnp.bfloat16)


def on_device(queries, key_tokens, value_tokens, pattern, w_out, out_gate):
    tok_rows, feat = queries.shape
    heads_here = feat // HEAD_DIM
    cubes_here = tok_rows // CUBE
    n_sel = pattern.shape[1]
    n_seq = lax.psum(1, "seq")
    me = lax.axis_index("seq")
    n_cubes = cubes_here * n_seq

    k3 = key_tokens.reshape(cubes_here, CUBE, feat)
    v3 = value_tokens.reshape(cubes_here, CUBE, feat)
    local_k = jnp.mean(k3.astype(jnp.float32), axis=1).astype(jnp.bfloat16)
    local_v = jnp.mean(v3.astype(jnp.float32), axis=1).astype(jnp.bfloat16)

    pat_all = lax.all_gather(pattern, "seq", axis=0, tiled=True)
    rows = pat_all.reshape(n_seq, cubes_here * n_sel)
    listed = jnp.any(rows[:, :, None] == jnp.arange(n_cubes, dtype=jnp.int32)[None, None, :], axis=1)
    listed = listed.reshape(n_seq, n_seq, cubes_here)

    need_by = lax.dynamic_index_in_dim(listed, me, axis=1, keepdims=False)
    pos_by = jnp.cumsum(need_by.astype(jnp.int32), axis=1) - 1
    hit = need_by[:, :, None] & (pos_by[:, :, None] == jnp.arange(CAP, dtype=jnp.int32)[None, None, :])
    send_idx = jnp.sum(jnp.where(hit, jnp.arange(cubes_here, dtype=jnp.int32)[None, :, None], 0), axis=1)

    kv_send = jnp.stack([k3[send_idx], v3[send_idx]], axis=2)
    kv_send = kv_send.reshape(n_seq, CAP * 2 * CUBE, feat)
    pooled_send = jnp.broadcast_to(
        jnp.concatenate([local_k, local_v], axis=0)[None], (n_seq, 2 * cubes_here, feat)
    )
    send = jnp.concatenate([kv_send, pooled_send], axis=1)
    recv = lax.all_to_all(send, "seq", 0, 0, tiled=True)

    kv_rows = CAP * 2 * CUBE
    pooled_k = recv[:, kv_rows:kv_rows + cubes_here, :].reshape(n_cubes, feat)
    pooled_v = recv[:, kv_rows + cubes_here:, :].reshape(n_cubes, feat)

    need_from = lax.dynamic_index_in_dim(listed, me, axis=0, keepdims=False)
    rank_from = jnp.cumsum(need_from.astype(jnp.int32), axis=1) - 1
    src = pattern // cubes_here
    loc = pattern % cubes_here
    remote_slot = cubes_here + src * CAP + rank_from[src, loc]
    tbl = jnp.where(src == me, loc, remote_slot).astype(jnp.int32)

    kern = functools.partial(attend_kernel, n_sel=n_sel, cubes_here=cubes_here, heads_here=heads_here)
    full3 = lambda i, t: (0, 0, 0)
    full2 = lambda i, t: (0, 0)
    attended = pl.pallas_call(
        kern,
        out_shape=jax.ShapeDtypeStruct((tok_rows, feat), jnp.bfloat16),
        grid_spec=pltpu.PrefetchScalarGridSpec(
            num_scalar_prefetch=1,
            grid=(cubes_here,),
            in_specs=[
                pl.BlockSpec((CUBE, feat), lambda i, t: (i, 0)),
                pl.BlockSpec((cubes_here, CUBE, feat), full3),
                pl.BlockSpec((cubes_here, CUBE, feat), full3),
                pl.BlockSpec(recv.shape, full3),
                pl.BlockSpec((n_cubes, feat), full2),
                pl.BlockSpec((n_cubes, feat), full2),
            ],
            out_specs=pl.BlockSpec((CUBE, feat), lambda i, t: (i, 0)),
            scratch_shapes=[
                pltpu.VMEM((n_sel * CUBE, feat), jnp.bfloat16),
                pltpu.VMEM((n_sel * CUBE, feat), jnp.bfloat16),
            ],
        ),
        compiler_params=pltpu.CompilerParams(vmem_limit_bytes=48 * 1024 * 1024),
    )(tbl, queries, k3, v3, recv, pooled_k, pooled_v)

    summed = lax.psum_scatter(
        jnp.dot(attended, w_out, preferred_element_type=jnp.float32).astype(jnp.bfloat16),
        "head",
        scatter_dimension=0,
        tiled=True,
    ).astype(jnp.float32)
    return (summed * out_gate[None, :]).astype(jnp.bfloat16)


def solution(mesh):
    return jax.shard_map(
        on_device,
        mesh=mesh,
        in_specs=(
            P("seq", "head"),
            P("seq", "head"),
            P("seq", "head"),
            P("seq", None),
            P("head", None),
            P(),
        ),
        out_specs=P(("seq", "head"), None),
        check_vma=False,
    )
```

```python
import functools

import jax
import jax.numpy as jnp
from jax import lax
from jax.experimental import pallas as pl
from jax.experimental.pallas import tpu as pltpu
from jax.sharding import Mesh, PartitionSpec as P

HEAD_DIM = 128
CUBE = 64
CAP = 6


def attend_kernel(tbl_ref, q_ref, ok_ref, ov_ref, rv_ref, pk_ref, pv_ref, o_ref, kbuf, vbuf,
                  *, n_sel, cubes_here, heads_here):
    i = pl.program_id(0)
    scale = HEAD_DIM ** (-0.5)

    def fill(j, carry):
        s = tbl_ref[i, j]
        dst = pl.ds(pl.multiple_of(j * CUBE, CUBE), CUBE)

        @pl.when(s < cubes_here)
        def _():
            kbuf[dst, :] = ok_ref[s]
            vbuf[dst, :] = ov_ref[s]

        @pl.when(s >= cubes_here)
        def _():
            t = s - cubes_here
            a = t // CAP
            base = pl.multiple_of((t % CAP) * (2 * CUBE), 2 * CUBE)
            kbuf[dst, :] = rv_ref[a, pl.ds(base, CUBE), :]
            vbuf[dst, :] = rv_ref[a, pl.ds(base + CUBE, CUBE), :]

        return carry

    lax.fori_loop(0, n_sel, fill, 0)

    def softmax_w(s):
        m = jnp.max(s, axis=-1, keepdims=True)
        p = jnp.exp(s - m)
        return (p / jnp.sum(p, axis=-1, keepdims=True)).astype(jnp.bfloat16)

    dims = (((1,), (1,)), ((), ()))
    for h in range(heads_here):
        cols = slice(h * HEAD_DIM, (h + 1) * HEAD_DIM)
        q = q_ref[:, cols]
        s_f = lax.dot_general(q, kbuf[:, cols], dims, preferred_element_type=jnp.float32) * scale
        fine = jnp.dot(softmax_w(s_f), vbuf[:, cols], preferred_element_type=jnp.float32)
        s_c = lax.dot_general(q, pk_ref[:, cols], dims, preferred_element_type=jnp.float32) * scale
        coarse = jnp.dot(softmax_w(s_c), pv_ref[:, cols], preferred_element_type=jnp.float32)
        o_ref[:, cols] = (fine + coarse).astype(jnp.bfloat16)


def on_device(queries, key_tokens, value_tokens, pattern, w_out, out_gate):
    tok_rows, feat = queries.shape
    heads_here = feat // HEAD_DIM
    cubes_here = tok_rows // CUBE
    n_sel = pattern.shape[1]
    n_seq = lax.psum(1, "seq")
    me = lax.axis_index("seq")
    n_cubes = cubes_here * n_seq

    k3 = key_tokens.reshape(cubes_here, CUBE, feat)
    v3 = value_tokens.reshape(cubes_here, CUBE, feat)
    local_k = jnp.mean(k3.astype(jnp.float32), axis=1).astype(jnp.bfloat16)
    local_v = jnp.mean(v3.astype(jnp.float32), axis=1).astype(jnp.bfloat16)

    listed_me = jnp.any(
        pattern.reshape(-1)[:, None] == jnp.arange(n_cubes, dtype=jnp.int32)[None, :], axis=0
    ).astype(jnp.int32).reshape(n_seq, cubes_here)
    need_by = lax.all_to_all(listed_me, "seq", 0, 0, tiled=True) > 0
    pos_by = jnp.cumsum(need_by.astype(jnp.int32), axis=1) - 1
    hit = need_by[:, :, None] & (pos_by[:, :, None] == jnp.arange(CAP, dtype=jnp.int32)[None, None, :])
    send_idx = jnp.sum(jnp.where(hit, jnp.arange(cubes_here, dtype=jnp.int32)[None, :, None], 0), axis=1)

    kv_send = jnp.stack([k3[send_idx], v3[send_idx]], axis=2)
    kv_send = kv_send.reshape(n_seq, CAP * 2 * CUBE, feat)
    pooled_send = jnp.broadcast_to(
        jnp.concatenate([local_k, local_v], axis=0)[None], (n_seq, 2 * cubes_here, feat)
    )
    send = jnp.concatenate([kv_send, pooled_send], axis=1)
    recv = lax.all_to_all(send, "seq", 0, 0, tiled=True)

    kv_rows = CAP * 2 * CUBE
    pooled_k = recv[:, kv_rows:kv_rows + cubes_here, :].reshape(n_cubes, feat)
    pooled_v = recv[:, kv_rows + cubes_here:, :].reshape(n_cubes, feat)

    rank_from = jnp.cumsum(listed_me, axis=1) - 1
    src = pattern // cubes_here
    loc = pattern % cubes_here
    remote_slot = cubes_here + src * CAP + rank_from[src, loc]
    tbl = jnp.where(src == me, loc, remote_slot).astype(jnp.int32)

    kern = functools.partial(attend_kernel, n_sel=n_sel, cubes_here=cubes_here, heads_here=heads_here)
    full3 = lambda i, t: (0, 0, 0)
    full2 = lambda i, t: (0, 0)
    attended = pl.pallas_call(
        kern,
        out_shape=jax.ShapeDtypeStruct((tok_rows, feat), jnp.bfloat16),
        grid_spec=pltpu.PrefetchScalarGridSpec(
            num_scalar_prefetch=1,
            grid=(cubes_here,),
            in_specs=[
                pl.BlockSpec((CUBE, feat), lambda i, t: (i, 0)),
                pl.BlockSpec((cubes_here, CUBE, feat), full3),
                pl.BlockSpec((cubes_here, CUBE, feat), full3),
                pl.BlockSpec(recv.shape, full3),
                pl.BlockSpec((n_cubes, feat), full2),
                pl.BlockSpec((n_cubes, feat), full2),
            ],
            out_specs=pl.BlockSpec((CUBE, feat), lambda i, t: (i, 0)),
            scratch_shapes=[
                pltpu.VMEM((n_sel * CUBE, feat), jnp.bfloat16),
                pltpu.VMEM((n_sel * CUBE, feat), jnp.bfloat16),
            ],
        ),
        compiler_params=pltpu.CompilerParams(vmem_limit_bytes=48 * 1024 * 1024),
    )(tbl, queries, k3, v3, recv, pooled_k, pooled_v)

    core = lax.axis_index("core")
    w_pair = lax.ppermute(w_out, "core", [(0, 1), (1, 0)])
    blocks = attended.reshape(tok_rows // (2 * CUBE), 2, CUBE, feat)
    mine = lax.dynamic_index_in_dim(blocks, core, axis=1, keepdims=False)
    theirs = lax.dynamic_index_in_dim(blocks, 1 - core, axis=1, keepdims=False)
    got = lax.ppermute(theirs, "core", [(0, 1), (1, 0)])
    own_term = jnp.dot(mine.reshape(-1, feat), w_out, preferred_element_type=jnp.float32)
    pair_term = jnp.dot(got.reshape(-1, feat), w_pair, preferred_element_type=jnp.float32)
    partial = (
        own_term.astype(jnp.bfloat16).astype(jnp.float32)
        + pair_term.astype(jnp.bfloat16).astype(jnp.float32)
    ).astype(jnp.bfloat16)
    summed = lax.psum_scatter(partial, "hx", scatter_dimension=0, tiled=True).astype(jnp.float32)
    return (summed * out_gate[None, :]).astype(jnp.bfloat16)


def solution(mesh):
    n_seq, n_head = mesh.devices.shape
    split = Mesh(mesh.devices.reshape(n_seq, n_head // 2, 2), ("seq", "hx", "core"))
    head = ("hx", "core")
    return jax.shard_map(
        on_device,
        mesh=split,
        in_specs=(
            P("seq", head),
            P("seq", head),
            P("seq", head),
            P("seq", None),
            P(head, None),
            P(),
        ),
        out_specs=P(("seq", "hx", "core"), None),
        check_vma=False,
    )
```

```python
import functools

import jax
import jax.numpy as jnp
from jax import lax
from jax.experimental import pallas as pl
from jax.experimental.pallas import tpu as pltpu
from jax.sharding import Mesh, PartitionSpec as P

HEAD_DIM = 128
CUBE = 64
CAP = 6


def attend_kernel(tbl_ref, q_ref, ok_ref, ov_ref, rv_ref, pk_ref, pv_ref, o_ref, kbuf, vbuf,
                  *, n_sel, cubes_here, heads_here):
    i = pl.program_id(0)
    scale = HEAD_DIM ** (-0.5)

    def fill(j, carry):
        s = tbl_ref[i, j]
        dst = pl.ds(pl.multiple_of(j * CUBE, CUBE), CUBE)

        @pl.when(s < cubes_here)
        def _():
            kbuf[dst, :] = ok_ref[s]
            vbuf[dst, :] = ov_ref[s]

        @pl.when(s >= cubes_here)
        def _():
            t = s - cubes_here
            a = t // CAP
            base = pl.multiple_of((t % CAP) * (2 * CUBE), 2 * CUBE)
            kbuf[dst, :] = rv_ref[a, pl.ds(base, CUBE), :]
            vbuf[dst, :] = rv_ref[a, pl.ds(base + CUBE, CUBE), :]

        return carry

    lax.fori_loop(0, n_sel, fill, 0)

    def softmax_w(s):
        m = jnp.max(s, axis=-1, keepdims=True)
        p = jnp.exp(s - m)
        return (p / jnp.sum(p, axis=-1, keepdims=True)).astype(jnp.bfloat16)

    dims = (((1,), (1,)), ((), ()))
    for h in range(heads_here):
        cols = slice(h * HEAD_DIM, (h + 1) * HEAD_DIM)
        q = q_ref[:, cols]
        s_f = lax.dot_general(q, kbuf[:, cols], dims, preferred_element_type=jnp.float32) * scale
        fine = jnp.dot(softmax_w(s_f), vbuf[:, cols], preferred_element_type=jnp.float32)
        s_c = lax.dot_general(q, pk_ref[:, cols], dims, preferred_element_type=jnp.float32) * scale
        coarse = jnp.dot(softmax_w(s_c), pv_ref[:, cols], preferred_element_type=jnp.float32)
        o_ref[:, cols] = (fine + coarse).astype(jnp.bfloat16)


def on_device(queries, key_tokens, value_tokens, pattern, w_out, out_gate):
    tok_rows, feat = queries.shape
    heads_here = feat // HEAD_DIM
    cubes_here = tok_rows // CUBE
    n_sel = pattern.shape[1]
    n_seq = lax.psum(1, "seq")
    me = lax.axis_index("seq")
    n_cubes = cubes_here * n_seq

    k3 = key_tokens.reshape(cubes_here, CUBE, feat)
    v3 = value_tokens.reshape(cubes_here, CUBE, feat)
    local_k = jnp.mean(k3.astype(jnp.float32), axis=1).astype(jnp.bfloat16)
    local_v = jnp.mean(v3.astype(jnp.float32), axis=1).astype(jnp.bfloat16)

    listed_me = jnp.any(
        pattern.reshape(-1)[:, None] == jnp.arange(n_cubes, dtype=jnp.int32)[None, :], axis=0
    ).astype(jnp.int32).reshape(n_seq, cubes_here)
    need_by = lax.all_to_all(listed_me, "seq", 0, 0, tiled=True) > 0
    pos_by = jnp.cumsum(need_by.astype(jnp.int32), axis=1) - 1
    hit = need_by[:, :, None] & (pos_by[:, :, None] == jnp.arange(CAP, dtype=jnp.int32)[None, None, :])
    send_idx = jnp.sum(jnp.where(hit, jnp.arange(cubes_here, dtype=jnp.int32)[None, :, None], 0), axis=1)

    kv_rows = CAP * 2 * CUBE
    source = jnp.concatenate(
        [jnp.concatenate([k3, v3], axis=1).reshape(cubes_here * 2 * CUBE, feat), local_k, local_v],
        axis=0,
    )
    cube_rows = send_idx[:, :, None] * (2 * CUBE) + jnp.arange(2 * CUBE, dtype=jnp.int32)[None, None, :]
    pooled_rows = cubes_here * 2 * CUBE + jnp.arange(2 * cubes_here, dtype=jnp.int32)
    row_idx = jnp.concatenate(
        [cube_rows.reshape(n_seq, kv_rows), jnp.broadcast_to(pooled_rows[None], (n_seq, 2 * cubes_here))],
        axis=1,
    )
    send = jnp.take(source, row_idx, axis=0)
    recv = lax.all_to_all(send, "seq", 0, 0, tiled=True)

    pooled_k = recv[:, kv_rows:kv_rows + cubes_here, :].reshape(n_cubes, feat)
    pooled_v = recv[:, kv_rows + cubes_here:, :].reshape(n_cubes, feat)

    rank_from = jnp.cumsum(listed_me, axis=1) - 1
    src = pattern // cubes_here
    loc = pattern % cubes_here
    remote_slot = cubes_here + src * CAP + rank_from[src, loc]
    tbl = jnp.where(src == me, loc, remote_slot).astype(jnp.int32)

    kern = functools.partial(attend_kernel, n_sel=n_sel, cubes_here=cubes_here, heads_here=heads_here)
    full3 = lambda i, t: (0, 0, 0)
    full2 = lambda i, t: (0, 0)
    attended = pl.pallas_call(
        kern,
        out_shape=jax.ShapeDtypeStruct((tok_rows, feat), jnp.bfloat16),
        grid_spec=pltpu.PrefetchScalarGridSpec(
            num_scalar_prefetch=1,
            grid=(cubes_here,),
            in_specs=[
                pl.BlockSpec((CUBE, feat), lambda i, t: (i, 0)),
                pl.BlockSpec((cubes_here, CUBE, feat), full3),
                pl.BlockSpec((cubes_here, CUBE, feat), full3),
                pl.BlockSpec(recv.shape, full3),
                pl.BlockSpec((n_cubes, feat), full2),
                pl.BlockSpec((n_cubes, feat), full2),
            ],
            out_specs=pl.BlockSpec((CUBE, feat), lambda i, t: (i, 0)),
            scratch_shapes=[
                pltpu.VMEM((n_sel * CUBE, feat), jnp.bfloat16),
                pltpu.VMEM((n_sel * CUBE, feat), jnp.bfloat16),
            ],
        ),
        compiler_params=pltpu.CompilerParams(vmem_limit_bytes=48 * 1024 * 1024),
    )(tbl, queries, k3, v3, recv, pooled_k, pooled_v)

    core = lax.axis_index("core")
    w_pair = lax.ppermute(w_out, "core", [(0, 1), (1, 0)])
    blocks = attended.reshape(tok_rows // (2 * CUBE), 2, CUBE, feat)
    mine = lax.dynamic_index_in_dim(blocks, core, axis=1, keepdims=False)
    theirs = lax.dynamic_index_in_dim(blocks, 1 - core, axis=1, keepdims=False)
    got = lax.ppermute(theirs, "core", [(0, 1), (1, 0)])
    own_term = jnp.dot(mine.reshape(-1, feat), w_out, preferred_element_type=jnp.float32)
    pair_term = jnp.dot(got.reshape(-1, feat), w_pair, preferred_element_type=jnp.float32)
    partial = (
        own_term.astype(jnp.bfloat16).astype(jnp.float32)
        + pair_term.astype(jnp.bfloat16).astype(jnp.float32)
    ).astype(jnp.bfloat16)
    n_hx = lax.psum(1, "hx")
    spread = lax.all_to_all(partial.reshape(n_hx, CUBE, -1), "hx", 0, 0, tiled=True)
    summed = jnp.sum(spread.astype(jnp.float32), axis=0)
    return (summed * out_gate[None, :]).astype(jnp.bfloat16)


def solution(mesh):
    n_seq, n_head = mesh.devices.shape
    split = Mesh(mesh.devices.reshape(n_seq, n_head // 2, 2), ("seq", "hx", "core"))
    head = ("hx", "core")
    return jax.shard_map(
        on_device,
        mesh=split,
        in_specs=(
            P("seq", head),
            P("seq", head),
            P("seq", head),
            P("seq", None),
            P(head, None),
            P(),
        ),
        out_specs=P(("seq", "hx", "core"), None),
        check_vma=False,
    )
```

```python
import functools

import jax
import jax.numpy as jnp
from jax import lax
from jax.experimental import pallas as pl
from jax.experimental.pallas import tpu as pltpu
from jax.sharding import Mesh, PartitionSpec as P

HEAD_DIM = 128
CUBE = 64
CAP = 6


def attend_kernel(tbl_ref, q_ref, ok_ref, ov_ref, rv_ref, pk_ref, pv_ref, o_ref, kbuf, vbuf,
                  *, n_sel, cubes_here, heads_here):
    i = pl.program_id(0)
    scale = HEAD_DIM ** (-0.5)

    def fill(j, carry):
        s = tbl_ref[i, j]
        dst = pl.ds(pl.multiple_of(j * CUBE, CUBE), CUBE)

        @pl.when(s < cubes_here)
        def _():
            kbuf[dst, :] = ok_ref[s]
            vbuf[dst, :] = ov_ref[s]

        @pl.when(s >= cubes_here)
        def _():
            t = s - cubes_here
            a = t // CAP
            base = pl.multiple_of((t % CAP) * (2 * CUBE), 2 * CUBE)
            kbuf[dst, :] = rv_ref[a, pl.ds(base, CUBE), :]
            vbuf[dst, :] = rv_ref[a, pl.ds(base + CUBE, CUBE), :]

        return carry

    lax.fori_loop(0, n_sel, fill, 0)

    def softmax_w(s):
        m = jnp.max(s, axis=-1, keepdims=True)
        p = jnp.exp(s - m)
        return (p / jnp.sum(p, axis=-1, keepdims=True)).astype(jnp.bfloat16)

    dims = (((1,), (1,)), ((), ()))
    for h in range(heads_here):
        cols = slice(h * HEAD_DIM, (h + 1) * HEAD_DIM)
        q = q_ref[:, cols]
        s_f = lax.dot_general(q, kbuf[:, cols], dims, preferred_element_type=jnp.float32) * scale
        fine = jnp.dot(softmax_w(s_f), vbuf[:, cols], preferred_element_type=jnp.float32)
        s_c = lax.dot_general(q, pk_ref[:, cols], dims, preferred_element_type=jnp.float32) * scale
        coarse = jnp.dot(softmax_w(s_c), pv_ref[:, cols], preferred_element_type=jnp.float32)
        o_ref[:, cols] = (fine + coarse).astype(jnp.bfloat16)


def pack_kernel(idx_ref, k_ref, v_ref, pooled_ref, o_ref, *, cubes_here):
    b = pl.program_id(0)
    for r in range(CAP):
        c = idx_ref[b, r]
        o_ref[pl.ds(r * 2 * CUBE, CUBE), :] = k_ref[c]
        o_ref[pl.ds(r * 2 * CUBE + CUBE, CUBE), :] = v_ref[c]
    o_ref[pl.ds(CAP * 2 * CUBE, 2 * cubes_here), :] = pooled_ref[...]


def on_device(queries, key_tokens, value_tokens, pattern, w_out, out_gate):
    tok_rows, feat = queries.shape
    heads_here = feat // HEAD_DIM
    cubes_here = tok_rows // CUBE
    n_sel = pattern.shape[1]
    n_seq = lax.psum(1, "seq")
    me = lax.axis_index("seq")
    n_cubes = cubes_here * n_seq

    k3 = key_tokens.reshape(cubes_here, CUBE, feat)
    v3 = value_tokens.reshape(cubes_here, CUBE, feat)
    local_k = jnp.mean(k3.astype(jnp.float32), axis=1).astype(jnp.bfloat16)
    local_v = jnp.mean(v3.astype(jnp.float32), axis=1).astype(jnp.bfloat16)

    listed_me = jnp.any(
        pattern.reshape(-1)[:, None] == jnp.arange(n_cubes, dtype=jnp.int32)[None, :], axis=0
    ).astype(jnp.int32).reshape(n_seq, cubes_here)
    need_by = lax.all_to_all(listed_me, "seq", 0, 0, tiled=True) > 0
    pos_by = jnp.cumsum(need_by.astype(jnp.int32), axis=1) - 1
    hit = need_by[:, :, None] & (pos_by[:, :, None] == jnp.arange(CAP, dtype=jnp.int32)[None, None, :])
    send_idx = jnp.sum(jnp.where(hit, jnp.arange(cubes_here, dtype=jnp.int32)[None, :, None], 0), axis=1)

    kv_rows = CAP * 2 * CUBE
    pooled = jnp.concatenate([local_k, local_v], axis=0)
    send = pl.pallas_call(
        functools.partial(pack_kernel, cubes_here=cubes_here),
        out_shape=jax.ShapeDtypeStruct((n_seq, kv_rows + 2 * cubes_here, feat), jnp.bfloat16),
        grid_spec=pltpu.PrefetchScalarGridSpec(
            num_scalar_prefetch=1,
            grid=(n_seq,),
            in_specs=[
                pl.BlockSpec((cubes_here, CUBE, feat), lambda b, t: (0, 0, 0)),
                pl.BlockSpec((cubes_here, CUBE, feat), lambda b, t: (0, 0, 0)),
                pl.BlockSpec((2 * cubes_here, feat), lambda b, t: (0, 0)),
            ],
            out_specs=pl.BlockSpec((None, kv_rows + 2 * cubes_here, feat), lambda b, t: (b, 0, 0)),
        ),
    )(send_idx, k3, v3, pooled)
    recv = lax.all_to_all(send, "seq", 0, 0, tiled=True)

    pooled_k = recv[:, kv_rows:kv_rows + cubes_here, :].reshape(n_cubes, feat)
    pooled_v = recv[:, kv_rows + cubes_here:, :].reshape(n_cubes, feat)

    rank_from = jnp.clip(jnp.cumsum(listed_me, axis=1) - 1, 0, CAP - 1)
    src = pattern // cubes_here
    loc = pattern % cubes_here
    remote_slot = cubes_here + src * CAP + rank_from[src, loc]
    tbl = jnp.where(src == me, loc, remote_slot).astype(jnp.int32)

    kern = functools.partial(attend_kernel, n_sel=n_sel, cubes_here=cubes_here, heads_here=heads_here)
    full3 = lambda i, t: (0, 0, 0)
    full2 = lambda i, t: (0, 0)
    attended = pl.pallas_call(
        kern,
        out_shape=jax.ShapeDtypeStruct((tok_rows, feat), jnp.bfloat16),
        grid_spec=pltpu.PrefetchScalarGridSpec(
            num_scalar_prefetch=1,
            grid=(cubes_here,),
            in_specs=[
                pl.BlockSpec((CUBE, feat), lambda i, t: (i, 0)),
                pl.BlockSpec((cubes_here, CUBE, feat), full3),
                pl.BlockSpec((cubes_here, CUBE, feat), full3),
                pl.BlockSpec(recv.shape, full3),
                pl.BlockSpec((n_cubes, feat), full2),
                pl.BlockSpec((n_cubes, feat), full2),
            ],
            out_specs=pl.BlockSpec((CUBE, feat), lambda i, t: (i, 0)),
            scratch_shapes=[
                pltpu.VMEM((n_sel * CUBE, feat), jnp.bfloat16),
                pltpu.VMEM((n_sel * CUBE, feat), jnp.bfloat16),
            ],
        ),
        compiler_params=pltpu.CompilerParams(vmem_limit_bytes=48 * 1024 * 1024),
    )(tbl, queries, k3, v3, recv, pooled_k, pooled_v)

    core = lax.axis_index("core")
    w_pair = lax.ppermute(w_out, "core", [(0, 1), (1, 0)])
    blocks = attended.reshape(tok_rows // (2 * CUBE), 2, CUBE, feat)
    mine = lax.dynamic_index_in_dim(blocks, core, axis=1, keepdims=False)
    theirs = lax.dynamic_index_in_dim(blocks, 1 - core, axis=1, keepdims=False)
    got = lax.ppermute(theirs, "core", [(0, 1), (1, 0)])
    own_term = jnp.dot(mine.reshape(-1, feat), w_out, preferred_element_type=jnp.float32)
    pair_term = jnp.dot(got.reshape(-1, feat), w_pair, preferred_element_type=jnp.float32)
    partial = (
        own_term.astype(jnp.bfloat16).astype(jnp.float32)
        + pair_term.astype(jnp.bfloat16).astype(jnp.float32)
    ).astype(jnp.bfloat16)
    n_hx = lax.psum(1, "hx")
    spread = lax.all_to_all(partial.reshape(n_hx, CUBE, -1), "hx", 0, 0, tiled=True)
    summed = jnp.sum(spread.astype(jnp.float32), axis=0)
    return (summed * out_gate[None, :]).astype(jnp.bfloat16)


def solution(mesh):
    n_seq, n_head = mesh.devices.shape
    split = Mesh(mesh.devices.reshape(n_seq, n_head // 2, 2), ("seq", "hx", "core"))
    head = ("hx", "core")
    return jax.shard_map(
        on_device,
        mesh=split,
        in_specs=(
            P("seq", head),
            P("seq", head),
            P("seq", head),
            P("seq", None),
            P(head, None),
            P(),
        ),
        out_specs=P(("seq", "hx", "core"), None),
        check_vma=False,
    )
```

```python
import functools

import jax
import jax.numpy as jnp
from jax import lax
from jax.experimental import pallas as pl
from jax.experimental.pallas import tpu as pltpu
from jax.sharding import Mesh, PartitionSpec as P

HEAD_DIM = 128
CUBE = 64
CAP = 6


def attend_kernel(src_ref, row_ref, q_ref, ok_hbm, ov_hbm, rv_hbm, pk_ref, pv_ref, o_ref,
                  kbuf, vbuf, sem, *, n_sel, heads_here):
    i = pl.program_id(0)
    steps = pl.num_programs(0)
    scale = HEAD_DIM ** (-0.5)

    def start(step, slot):
        for j in range(n_sel):
            a = src_ref[step, j]
            r = row_ref[step, j]
            dst = pl.ds(j * CUBE, CUBE)

            @pl.when(a < 0)
            def _():
                pltpu.make_async_copy(ok_hbm.at[r], kbuf.at[slot, dst], sem.at[0, slot]).start()
                pltpu.make_async_copy(ov_hbm.at[r], vbuf.at[slot, dst], sem.at[1, slot]).start()

            @pl.when(a >= 0)
            def _():
                base = pl.multiple_of(r, 2 * CUBE)
                pltpu.make_async_copy(
                    rv_hbm.at[a, pl.ds(base, CUBE)], kbuf.at[slot, dst], sem.at[0, slot]).start()
                pltpu.make_async_copy(
                    rv_hbm.at[a, pl.ds(base + CUBE, CUBE)], vbuf.at[slot, dst], sem.at[1, slot]).start()

    @pl.when(i == 0)
    def _():
        start(0, 0)

    slot = i % 2

    @pl.when(i + 1 < steps)
    def _():
        start(i + 1, 1 - slot)

    pltpu.make_async_copy(kbuf.at[slot], kbuf.at[slot], sem.at[0, slot]).wait()
    pltpu.make_async_copy(vbuf.at[slot], vbuf.at[slot], sem.at[1, slot]).wait()

    def softmax_w(s):
        m = jnp.max(s, axis=-1, keepdims=True)
        p = jnp.exp(s - m)
        return (p / jnp.sum(p, axis=-1, keepdims=True)).astype(jnp.bfloat16)

    dims = (((1,), (1,)), ((), ()))
    for h in range(heads_here):
        cols = slice(h * HEAD_DIM, (h + 1) * HEAD_DIM)
        q = q_ref[:, cols]
        s_f = lax.dot_general(q, kbuf[slot, :, cols], dims, preferred_element_type=jnp.float32) * scale
        fine = jnp.dot(softmax_w(s_f), vbuf[slot, :, cols], preferred_element_type=jnp.float32)
        s_c = lax.dot_general(q, pk_ref[:, cols], dims, preferred_element_type=jnp.float32) * scale
        coarse = jnp.dot(softmax_w(s_c), pv_ref[:, cols], preferred_element_type=jnp.float32)
        o_ref[:, cols] = (fine + coarse).astype(jnp.bfloat16)


def pack_kernel(idx_ref, k_ref, v_ref, pooled_ref, o_ref, *, cubes_here):
    b = pl.program_id(0)
    for r in range(CAP):
        c = idx_ref[b, r]
        o_ref[pl.ds(r * 2 * CUBE, CUBE), :] = k_ref[c]
        o_ref[pl.ds(r * 2 * CUBE + CUBE, CUBE), :] = v_ref[c]
    o_ref[pl.ds(CAP * 2 * CUBE, 2 * cubes_here), :] = pooled_ref[...]


def on_device(queries, key_tokens, value_tokens, pattern, w_out, out_gate):
    tok_rows, feat = queries.shape
    heads_here = feat // HEAD_DIM
    cubes_here = tok_rows // CUBE
    n_sel = pattern.shape[1]
    n_seq = lax.psum(1, "seq")
    me = lax.axis_index("seq")
    n_cubes = cubes_here * n_seq

    k3 = key_tokens.reshape(cubes_here, CUBE, feat)
    v3 = value_tokens.reshape(cubes_here, CUBE, feat)
    local_k = jnp.mean(k3.astype(jnp.float32), axis=1).astype(jnp.bfloat16)
    local_v = jnp.mean(v3.astype(jnp.float32), axis=1).astype(jnp.bfloat16)

    listed_me = jnp.any(
        pattern.reshape(-1)[:, None] == jnp.arange(n_cubes, dtype=jnp.int32)[None, :], axis=0
    ).astype(jnp.int32).reshape(n_seq, cubes_here)
    need_by = lax.all_to_all(listed_me, "seq", 0, 0, tiled=True) > 0
    pos_by = jnp.cumsum(need_by.astype(jnp.int32), axis=1) - 1
    hit = need_by[:, :, None] & (pos_by[:, :, None] == jnp.arange(CAP, dtype=jnp.int32)[None, None, :])
    send_idx = jnp.sum(jnp.where(hit, jnp.arange(cubes_here, dtype=jnp.int32)[None, :, None], 0), axis=1)

    kv_rows = CAP * 2 * CUBE
    pooled = jnp.concatenate([local_k, local_v], axis=0)
    send = pl.pallas_call(
        functools.partial(pack_kernel, cubes_here=cubes_here),
        out_shape=jax.ShapeDtypeStruct((n_seq, kv_rows + 2 * cubes_here, feat), jnp.bfloat16),
        grid_spec=pltpu.PrefetchScalarGridSpec(
            num_scalar_prefetch=1,
            grid=(n_seq,),
            in_specs=[
                pl.BlockSpec((cubes_here, CUBE, feat), lambda b, t: (0, 0, 0)),
                pl.BlockSpec((cubes_here, CUBE, feat), lambda b, t: (0, 0, 0)),
                pl.BlockSpec((2 * cubes_here, feat), lambda b, t: (0, 0)),
            ],
            out_specs=pl.BlockSpec((None, kv_rows + 2 * cubes_here, feat), lambda b, t: (b, 0, 0)),
        ),
    )(send_idx, k3, v3, pooled)
    recv = lax.all_to_all(send, "seq", 0, 0, tiled=True)

    pooled_k = recv[:, kv_rows:kv_rows + cubes_here, :].reshape(n_cubes, feat)
    pooled_v = recv[:, kv_rows + cubes_here:, :].reshape(n_cubes, feat)

    rank_from = jnp.clip(jnp.cumsum(listed_me, axis=1) - 1, 0, CAP - 1)
    src = pattern // cubes_here
    loc = pattern % cubes_here
    own = src == me
    src_tbl = jnp.where(own, -1, src).astype(jnp.int32)
    row_tbl = jnp.where(own, loc, rank_from[src, loc] * (2 * CUBE)).astype(jnp.int32)

    kern = functools.partial(attend_kernel, n_sel=n_sel, heads_here=heads_here)
    full2 = lambda i, a, r: (0, 0)
    hbm = pl.BlockSpec(memory_space=pl.ANY)
    attended = pl.pallas_call(
        kern,
        out_shape=jax.ShapeDtypeStruct((tok_rows, feat), jnp.bfloat16),
        grid_spec=pltpu.PrefetchScalarGridSpec(
            num_scalar_prefetch=2,
            grid=(cubes_here,),
            in_specs=[
                pl.BlockSpec((CUBE, feat), lambda i, a, r: (i, 0)),
                hbm,
                hbm,
                hbm,
                pl.BlockSpec((n_cubes, feat), full2),
                pl.BlockSpec((n_cubes, feat), full2),
            ],
            out_specs=pl.BlockSpec((CUBE, feat), lambda i, a, r: (i, 0)),
            scratch_shapes=[
                pltpu.VMEM((2, n_sel * CUBE, feat), jnp.bfloat16),
                pltpu.VMEM((2, n_sel * CUBE, feat), jnp.bfloat16),
                pltpu.SemaphoreType.DMA((2, 2)),
            ],
        ),
        compiler_params=pltpu.CompilerParams(
            dimension_semantics=("arbitrary",), vmem_limit_bytes=32 * 1024 * 1024),
    )(src_tbl, row_tbl, queries, k3, v3, recv, pooled_k, pooled_v)

    core = lax.axis_index("core")
    w_pair = lax.ppermute(w_out, "core", [(0, 1), (1, 0)])
    blocks = attended.reshape(tok_rows // (2 * CUBE), 2, CUBE, feat)
    mine = lax.dynamic_index_in_dim(blocks, core, axis=1, keepdims=False)
    theirs = lax.dynamic_index_in_dim(blocks, 1 - core, axis=1, keepdims=False)
    got = lax.ppermute(theirs, "core", [(0, 1), (1, 0)])
    own_term = jnp.dot(mine.reshape(-1, feat), w_out, preferred_element_type=jnp.float32)
    pair_term = jnp.dot(got.reshape(-1, feat), w_pair, preferred_element_type=jnp.float32)
    partial = (
        own_term.astype(jnp.bfloat16).astype(jnp.float32)
        + pair_term.astype(jnp.bfloat16).astype(jnp.float32)
    ).astype(jnp.bfloat16)
    n_hx = lax.psum(1, "hx")
    spread = lax.all_to_all(partial.reshape(n_hx, CUBE, -1), "hx", 0, 0, tiled=True)
    summed = jnp.sum(spread.astype(jnp.float32), axis=0)
    return (summed * out_gate[None, :]).astype(jnp.bfloat16)


def solution(mesh):
    n_seq, n_head = mesh.devices.shape
    split = Mesh(mesh.devices.reshape(n_seq, n_head // 2, 2), ("seq", "hx", "core"))
    head = ("hx", "core")
    return jax.shard_map(
        on_device,
        mesh=split,
        in_specs=(
            P("seq", head),
            P("seq", head),
            P("seq", head),
            P("seq", None),
            P(head, None),
            P(),
        ),
        out_specs=P(("seq", "hx", "core"), None),
        check_vma=False,
    )
```

```python
import functools

import jax
import jax.numpy as jnp
from jax import lax
from jax.experimental import pallas as pl
from jax.experimental.pallas import tpu as pltpu
from jax.sharding import Mesh, PartitionSpec as P

HEAD_DIM = 128
CUBE = 64
CAP = 6


def attend_kernel(src_ref, row_ref, q_ref, okv_hbm, rv_hbm, pk_ref, pv_ref, o_ref,
                  kvbuf, sem, *, n_sel, heads_here):
    i = pl.program_id(0)
    steps = pl.num_programs(0)
    scale = HEAD_DIM ** (-0.5)

    def start(step, slot):
        for j in range(n_sel):
            a = src_ref[step, j]
            r = row_ref[step, j]

            @pl.when(a < 0)
            def _():
                pltpu.make_async_copy(okv_hbm.at[r], kvbuf.at[slot, j], sem.at[slot]).start()

            @pl.when(a >= 0)
            def _():
                base = pl.multiple_of(r, 2 * CUBE)
                pltpu.make_async_copy(
                    rv_hbm.at[a, pl.ds(base, 2 * CUBE)], kvbuf.at[slot, j], sem.at[slot]).start()

    @pl.when(i == 0)
    def _():
        start(0, 0)

    slot = i % 2

    @pl.when(i + 1 < steps)
    def _():
        start(i + 1, 1 - slot)

    pltpu.make_async_copy(kvbuf.at[slot], kvbuf.at[slot], sem.at[slot]).wait()

    def softmax_w(s):
        m = jnp.max(s, axis=-1, keepdims=True)
        p = jnp.exp(s - m)
        return (p / jnp.sum(p, axis=-1, keepdims=True)).astype(jnp.bfloat16)

    dims = (((1,), (1,)), ((), ()))
    for h in range(heads_here):
        cols = slice(h * HEAD_DIM, (h + 1) * HEAD_DIM)
        q = q_ref[:, cols]
        k = kvbuf[slot, :, pl.ds(0, CUBE), cols].reshape(n_sel * CUBE, HEAD_DIM)
        v = kvbuf[slot, :, pl.ds(CUBE, CUBE), cols].reshape(n_sel * CUBE, HEAD_DIM)
        s_f = lax.dot_general(q, k, dims, preferred_element_type=jnp.float32) * scale
        fine = jnp.dot(softmax_w(s_f), v, preferred_element_type=jnp.float32)
        s_c = lax.dot_general(q, pk_ref[:, cols], dims, preferred_element_type=jnp.float32) * scale
        coarse = jnp.dot(softmax_w(s_c), pv_ref[:, cols], preferred_element_type=jnp.float32)
        o_ref[:, cols] = (fine + coarse).astype(jnp.bfloat16)


def pack_kernel(idx_ref, k_ref, v_ref, pooled_ref, o_ref, *, cubes_here):
    b = pl.program_id(0)
    for r in range(CAP):
        c = idx_ref[b, r]
        o_ref[pl.ds(r * 2 * CUBE, CUBE), :] = k_ref[c]
        o_ref[pl.ds(r * 2 * CUBE + CUBE, CUBE), :] = v_ref[c]
    o_ref[pl.ds(CAP * 2 * CUBE, 2 * cubes_here), :] = pooled_ref[...]


def on_device(queries, key_tokens, value_tokens, pattern, w_out, out_gate):
    tok_rows, feat = queries.shape
    heads_here = feat // HEAD_DIM
    cubes_here = tok_rows // CUBE
    n_sel = pattern.shape[1]
    n_seq = lax.psum(1, "seq")
    me = lax.axis_index("seq")
    n_cubes = cubes_here * n_seq

    k3 = key_tokens.reshape(cubes_here, CUBE, feat)
    v3 = value_tokens.reshape(cubes_here, CUBE, feat)
    local_k = jnp.mean(k3.astype(jnp.float32), axis=1).astype(jnp.bfloat16)
    local_v = jnp.mean(v3.astype(jnp.float32), axis=1).astype(jnp.bfloat16)

    listed_me = jnp.any(
        pattern.reshape(-1)[:, None] == jnp.arange(n_cubes, dtype=jnp.int32)[None, :], axis=0
    ).astype(jnp.int32).reshape(n_seq, cubes_here)
    need_by = lax.all_to_all(listed_me, "seq", 0, 0, tiled=True) > 0
    pos_by = jnp.cumsum(need_by.astype(jnp.int32), axis=1) - 1
    hit = need_by[:, :, None] & (pos_by[:, :, None] == jnp.arange(CAP, dtype=jnp.int32)[None, None, :])
    send_idx = jnp.sum(jnp.where(hit, jnp.arange(cubes_here, dtype=jnp.int32)[None, :, None], 0), axis=1)

    kv_rows = CAP * 2 * CUBE
    pooled = jnp.concatenate([local_k, local_v], axis=0)
    send = pl.pallas_call(
        functools.partial(pack_kernel, cubes_here=cubes_here),
        out_shape=jax.ShapeDtypeStruct((n_seq, kv_rows + 2 * cubes_here, feat), jnp.bfloat16),
        grid_spec=pltpu.PrefetchScalarGridSpec(
            num_scalar_prefetch=1,
            grid=(n_seq,),
            in_specs=[
                pl.BlockSpec((cubes_here, CUBE, feat), lambda b, t: (0, 0, 0)),
                pl.BlockSpec((cubes_here, CUBE, feat), lambda b, t: (0, 0, 0)),
                pl.BlockSpec((2 * cubes_here, feat), lambda b, t: (0, 0)),
            ],
            out_specs=pl.BlockSpec((None, kv_rows + 2 * cubes_here, feat), lambda b, t: (b, 0, 0)),
        ),
    )(send_idx, k3, v3, pooled)
    recv = lax.all_to_all(send, "seq", 0, 0, tiled=True)

    pooled_k = recv[:, kv_rows:kv_rows + cubes_here, :].reshape(n_cubes, feat)
    pooled_v = recv[:, kv_rows + cubes_here:, :].reshape(n_cubes, feat)

    rank_from = jnp.clip(jnp.cumsum(listed_me, axis=1) - 1, 0, CAP - 1)
    src = pattern // cubes_here
    loc = pattern % cubes_here
    own = src == me
    src_tbl = jnp.where(own, -1, src).astype(jnp.int32)
    row_tbl = jnp.where(own, loc, rank_from[src, loc] * (2 * CUBE)).astype(jnp.int32)

    kern = functools.partial(attend_kernel, n_sel=n_sel, heads_here=heads_here)
    full2 = lambda i, a, r: (0, 0)
    hbm = pl.BlockSpec(memory_space=pl.ANY)
    attended = pl.pallas_call(
        kern,
        out_shape=jax.ShapeDtypeStruct((tok_rows, feat), jnp.bfloat16),
        grid_spec=pltpu.PrefetchScalarGridSpec(
            num_scalar_prefetch=2,
            grid=(cubes_here,),
            in_specs=[
                pl.BlockSpec((CUBE, feat), lambda i, a, r: (i, 0)),
                hbm,
                hbm,
                pl.BlockSpec((n_cubes, feat), full2),
                pl.BlockSpec((n_cubes, feat), full2),
            ],
            out_specs=pl.BlockSpec((CUBE, feat), lambda i, a, r: (i, 0)),
            scratch_shapes=[
                pltpu.VMEM((2, n_sel, 2 * CUBE, feat), jnp.bfloat16),
                pltpu.SemaphoreType.DMA((2,)),
            ],
        ),
        compiler_params=pltpu.CompilerParams(
            dimension_semantics=("arbitrary",), vmem_limit_bytes=32 * 1024 * 1024),
    )(src_tbl, row_tbl, queries, jnp.concatenate([k3, v3], axis=1), recv, pooled_k, pooled_v)

    core = lax.axis_index("core")
    w_pair = lax.ppermute(w_out, "core", [(0, 1), (1, 0)])
    blocks = attended.reshape(tok_rows // (2 * CUBE), 2, CUBE, feat)
    mine = lax.dynamic_index_in_dim(blocks, core, axis=1, keepdims=False)
    theirs = lax.dynamic_index_in_dim(blocks, 1 - core, axis=1, keepdims=False)
    got = lax.ppermute(theirs, "core", [(0, 1), (1, 0)])
    own_term = jnp.dot(mine.reshape(-1, feat), w_out, preferred_element_type=jnp.float32)
    pair_term = jnp.dot(got.reshape(-1, feat), w_pair, preferred_element_type=jnp.float32)
    partial = (
        own_term.astype(jnp.bfloat16).astype(jnp.float32)
        + pair_term.astype(jnp.bfloat16).astype(jnp.float32)
    ).astype(jnp.bfloat16)
    n_hx = lax.psum(1, "hx")
    spread = lax.all_to_all(partial.reshape(n_hx, CUBE, -1), "hx", 0, 0, tiled=True)
    summed = jnp.sum(spread.astype(jnp.float32), axis=0)
    return (summed * out_gate[None, :]).astype(jnp.bfloat16)


def solution(mesh):
    n_seq, n_head = mesh.devices.shape
    split = Mesh(mesh.devices.reshape(n_seq, n_head // 2, 2), ("seq", "hx", "core"))
    head = ("hx", "core")
    return jax.shard_map(
        on_device,
        mesh=split,
        in_specs=(
            P("seq", head),
            P("seq", head),
            P("seq", head),
            P("seq", None),
            P(head, None),
            P(),
        ),
        out_specs=P(("seq", "hx", "core"), None),
        check_vma=False,
    )
```

```python
import functools

import jax
import jax.numpy as jnp
from jax import lax
from jax.experimental import pallas as pl
from jax.experimental.pallas import tpu as pltpu
from jax.sharding import Mesh, PartitionSpec as P

HEAD_DIM = 128
CUBE = 64
CAP = 6


def attend_kernel(src_ref, row_ref, q_ref, okv_hbm, rv_hbm, pk_ref, pv_ref, o_ref,
                  kvbuf, sem, *, n_sel, heads_here):
    i = pl.program_id(0)
    steps = pl.num_programs(0)
    scale = HEAD_DIM ** (-0.5)

    def start(step, slot):
        for j in range(n_sel):
            a = src_ref[step, j]
            r = row_ref[step, j]

            @pl.when(a < 0)
            def _():
                pltpu.make_async_copy(okv_hbm.at[r], kvbuf.at[slot, j], sem.at[slot]).start()

            @pl.when(a >= 0)
            def _():
                base = pl.multiple_of(r, 2 * CUBE)
                pltpu.make_async_copy(
                    rv_hbm.at[a, pl.ds(base, 2 * CUBE)], kvbuf.at[slot, j], sem.at[slot]).start()

    @pl.when(i == 0)
    def _():
        start(0, 0)

    slot = i % 2

    @pl.when(i + 1 < steps)
    def _():
        start(i + 1, 1 - slot)

    pltpu.make_async_copy(kvbuf.at[slot], kvbuf.at[slot], sem.at[slot]).wait()

    def softmax_w(s):
        m = jnp.max(s, axis=-1, keepdims=True)
        p = jnp.exp(s - m)
        return (p / jnp.sum(p, axis=-1, keepdims=True)).astype(jnp.bfloat16)

    dims = (((1,), (1,)), ((), ()))
    for h in range(heads_here):
        cols = slice(h * HEAD_DIM, (h + 1) * HEAD_DIM)
        q = q_ref[:, cols]
        k = kvbuf[slot, :, pl.ds(0, CUBE), cols].reshape(n_sel * CUBE, HEAD_DIM)
        v = kvbuf[slot, :, pl.ds(CUBE, CUBE), cols].reshape(n_sel * CUBE, HEAD_DIM)
        s_f = lax.dot_general(q, k, dims, preferred_element_type=jnp.float32) * scale
        fine = jnp.dot(softmax_w(s_f), v, preferred_element_type=jnp.float32)
        s_c = lax.dot_general(q, pk_ref[:, cols], dims, preferred_element_type=jnp.float32) * scale
        coarse = jnp.dot(softmax_w(s_c), pv_ref[:, cols], preferred_element_type=jnp.float32)
        o_ref[:, cols] = (fine + coarse).astype(jnp.bfloat16)


def pack_kernel(idx_ref, k_ref, v_ref, pooled_ref, o_ref, *, cubes_here):
    b = pl.program_id(0)
    for r in range(CAP):
        c = idx_ref[b, r]
        o_ref[pl.ds(r * 2 * CUBE, CUBE), :] = k_ref[c]
        o_ref[pl.ds(r * 2 * CUBE + CUBE, CUBE), :] = v_ref[c]
    o_ref[pl.ds(CAP * 2 * CUBE, 2 * cubes_here), :] = pooled_ref[...]


def on_device(queries, key_tokens, value_tokens, pattern, w_out, out_gate):
    tok_rows, feat = queries.shape
    heads_here = feat // HEAD_DIM
    cubes_here = tok_rows // CUBE
    n_sel = pattern.shape[1]
    n_seq = lax.psum(1, "seq")
    me = lax.axis_index("seq")
    n_cubes = cubes_here * n_seq

    k3 = key_tokens.reshape(cubes_here, CUBE, feat)
    v3 = value_tokens.reshape(cubes_here, CUBE, feat)
    local_k = jnp.mean(k3.astype(jnp.float32), axis=1).astype(jnp.bfloat16)
    local_v = jnp.mean(v3.astype(jnp.float32), axis=1).astype(jnp.bfloat16)

    listed_me = jnp.any(
        pattern.reshape(-1)[:, None] == jnp.arange(n_cubes, dtype=jnp.int32)[None, :], axis=0
    ).astype(jnp.int32).reshape(n_seq, cubes_here)
    need_by = lax.all_to_all(listed_me, "seq", 0, 0, tiled=True) > 0
    pos_by = jnp.cumsum(need_by.astype(jnp.int32), axis=1) - 1
    hit = need_by[:, :, None] & (pos_by[:, :, None] == jnp.arange(CAP, dtype=jnp.int32)[None, None, :])
    send_idx = jnp.sum(jnp.where(hit, jnp.arange(cubes_here, dtype=jnp.int32)[None, :, None], 0), axis=1)

    kv_rows = CAP * 2 * CUBE
    pooled = jnp.concatenate([local_k, local_v], axis=0)
    send = pl.pallas_call(
        functools.partial(pack_kernel, cubes_here=cubes_here),
        out_shape=jax.ShapeDtypeStruct((n_seq, kv_rows + 2 * cubes_here, feat), jnp.bfloat16),
        grid_spec=pltpu.PrefetchScalarGridSpec(
            num_scalar_prefetch=1,
            grid=(n_seq,),
            in_specs=[
                pl.BlockSpec((cubes_here, CUBE, feat), lambda b, t: (0, 0, 0)),
                pl.BlockSpec((cubes_here, CUBE, feat), lambda b, t: (0, 0, 0)),
                pl.BlockSpec((2 * cubes_here, feat), lambda b, t: (0, 0)),
            ],
            out_specs=pl.BlockSpec((None, kv_rows + 2 * cubes_here, feat), lambda b, t: (b, 0, 0)),
        ),
    )(send_idx, k3, v3, pooled)
    recv = lax.all_to_all(send, "seq", 0, 0, tiled=True)

    pooled_k = recv[:, kv_rows:kv_rows + cubes_here, :].reshape(n_cubes, feat)
    pooled_v = recv[:, kv_rows + cubes_here:, :].reshape(n_cubes, feat)

    rank_from = jnp.clip(jnp.cumsum(listed_me, axis=1) - 1, 0, CAP - 1)
    src = pattern // cubes_here
    loc = pattern % cubes_here
    own = src == me
    src_tbl = jnp.where(own, -1, src).astype(jnp.int32)
    row_tbl = jnp.where(own, loc, rank_from[src, loc] * (2 * CUBE)).astype(jnp.int32)

    kern = functools.partial(attend_kernel, n_sel=n_sel, heads_here=heads_here)
    full2 = lambda i, a, r: (0, 0)
    hbm = pl.BlockSpec(memory_space=pl.ANY)
    attended = pl.pallas_call(
        kern,
        out_shape=jax.ShapeDtypeStruct((tok_rows, feat), jnp.bfloat16),
        grid_spec=pltpu.PrefetchScalarGridSpec(
            num_scalar_prefetch=2,
            grid=(cubes_here,),
            in_specs=[
                pl.BlockSpec((CUBE, feat), lambda i, a, r: (i, 0)),
                hbm,
                hbm,
                pl.BlockSpec((n_cubes, feat), full2),
                pl.BlockSpec((n_cubes, feat), full2),
            ],
            out_specs=pl.BlockSpec((CUBE, feat), lambda i, a, r: (i, 0)),
            scratch_shapes=[
                pltpu.VMEM((2, n_sel, 2 * CUBE, feat), jnp.bfloat16),
                pltpu.SemaphoreType.DMA((2,)),
            ],
        ),
        compiler_params=pltpu.CompilerParams(
            dimension_semantics=("arbitrary",), vmem_limit_bytes=32 * 1024 * 1024),
    )(src_tbl, row_tbl, queries, jnp.concatenate([k3, v3], axis=1), recv, pooled_k, pooled_v)

    pair = ("yh", "core")
    n_pair = lax.psum(1, pair)
    n_x = lax.psum(1, "x")
    w_all = lax.all_gather(w_out, pair, axis=0, tiled=True)
    per_dest = attended.reshape(-1, n_x, 2, CUBE, feat)
    per_dest = jnp.transpose(per_dest, (0, 2, 1, 3, 4)).reshape(n_pair, n_x * CUBE, feat)
    got = lax.all_to_all(per_dest, pair, 0, 0, tiled=True)
    partial = None
    for g in range(n_pair):
        term = jnp.dot(got[g], w_all[g * feat:(g + 1) * feat], preferred_element_type=jnp.float32)
        term = term.astype(jnp.bfloat16).astype(jnp.float32)
        partial = term if partial is None else partial + term
    spread = lax.all_to_all(partial.astype(jnp.bfloat16).reshape(n_x, CUBE, -1), "x", 0, 0, tiled=True)
    summed = jnp.sum(spread.astype(jnp.float32), axis=0)
    return (summed * out_gate[None, :]).astype(jnp.bfloat16)


def solution(mesh):
    n_seq, n_head = mesh.devices.shape
    split = Mesh(mesh.devices.reshape(n_seq, 2, n_head // 4, 2), ("seq", "yh", "x", "core"))
    head = ("yh", "x", "core")
    return jax.shard_map(
        on_device,
        mesh=split,
        in_specs=(
            P("seq", head),
            P("seq", head),
            P("seq", head),
            P("seq", None),
            P(head, None),
            P(),
        ),
        out_specs=P(("seq", "yh", "x", "core"), None),
        check_vma=False,
    )
```

```python
import functools

import jax
import jax.numpy as jnp
from jax import lax
from jax.experimental import pallas as pl
from jax.experimental.pallas import tpu as pltpu
from jax.sharding import Mesh, PartitionSpec as P

HEAD_DIM = 128
CUBE = 64
CAP = 6


def attend_kernel(src_ref, row_ref, q_ref, okv_hbm, rv_hbm, pk_ref, pv_ref, o_ref,
                  kvbuf, sem, *, n_sel, head):
    i = pl.program_id(0)
    steps = pl.num_programs(0)
    scale = HEAD_DIM ** (-0.5)

    def start(step, slot):
        for j in range(n_sel):
            a = src_ref[step, j]
            r = row_ref[step, j]

            @pl.when(a < 0)
            def _():
                pltpu.make_async_copy(
                    okv_hbm.at[r, :, pl.ds(head * HEAD_DIM, HEAD_DIM)], kvbuf.at[slot, j], sem.at[slot]).start()

            @pl.when(a >= 0)
            def _():
                base = pl.multiple_of(r, 2 * CUBE)
                pltpu.make_async_copy(
                    rv_hbm.at[a, pl.ds(base, 2 * CUBE)], kvbuf.at[slot, j], sem.at[slot]).start()

    @pl.when(i == 0)
    def _():
        start(0, 0)

    slot = i % 2

    @pl.when(i + 1 < steps)
    def _():
        start(i + 1, 1 - slot)

    pltpu.make_async_copy(kvbuf.at[slot], kvbuf.at[slot], sem.at[slot]).wait()

    def softmax_w(s):
        m = jnp.max(s, axis=-1, keepdims=True)
        p = jnp.exp(s - m)
        return (p / jnp.sum(p, axis=-1, keepdims=True)).astype(jnp.bfloat16)

    dims = (((1,), (1,)), ((), ()))
    q = q_ref[...]
    k = kvbuf[slot, :, pl.ds(0, CUBE), :].reshape(n_sel * CUBE, HEAD_DIM)
    v = kvbuf[slot, :, pl.ds(CUBE, CUBE), :].reshape(n_sel * CUBE, HEAD_DIM)
    s_f = lax.dot_general(q, k, dims, preferred_element_type=jnp.float32) * scale
    fine = jnp.dot(softmax_w(s_f), v, preferred_element_type=jnp.float32)
    s_c = lax.dot_general(q, pk_ref[...], dims, preferred_element_type=jnp.float32) * scale
    coarse = jnp.dot(softmax_w(s_c), pv_ref[...], preferred_element_type=jnp.float32)
    o_ref[...] = (fine + coarse).astype(jnp.bfloat16)


def pack_kernel(idx_ref, k_ref, v_ref, pooled_ref, *o_refs, cubes_here):
    b = pl.program_id(0)
    for h, o_ref in enumerate(o_refs):
        cols = pl.ds(h * HEAD_DIM, HEAD_DIM)
        for r in range(CAP):
            c = idx_ref[b, r]
            o_ref[pl.ds(r * 2 * CUBE, CUBE), :] = k_ref[c, :, cols]
            o_ref[pl.ds(r * 2 * CUBE + CUBE, CUBE), :] = v_ref[c, :, cols]
        o_ref[pl.ds(CAP * 2 * CUBE, 2 * cubes_here), :] = pooled_ref[:, cols]


def on_device(queries, key_tokens, value_tokens, pattern, w_out, out_gate):
    tok_rows, feat = queries.shape
    heads_here = feat // HEAD_DIM
    cubes_here = tok_rows // CUBE
    n_sel = pattern.shape[1]
    n_seq = lax.psum(1, "seq")
    me = lax.axis_index("seq")
    n_cubes = cubes_here * n_seq

    k3 = key_tokens.reshape(cubes_here, CUBE, feat)
    v3 = value_tokens.reshape(cubes_here, CUBE, feat)
    local_k = jnp.mean(k3.astype(jnp.float32), axis=1).astype(jnp.bfloat16)
    local_v = jnp.mean(v3.astype(jnp.float32), axis=1).astype(jnp.bfloat16)

    listed_me = jnp.any(
        pattern.reshape(-1)[:, None] == jnp.arange(n_cubes, dtype=jnp.int32)[None, :], axis=0
    ).astype(jnp.int32).reshape(n_seq, cubes_here)
    need_by = lax.all_to_all(listed_me, "seq", 0, 0, tiled=True) > 0
    pos_by = jnp.cumsum(need_by.astype(jnp.int32), axis=1) - 1
    hit = need_by[:, :, None] & (pos_by[:, :, None] == jnp.arange(CAP, dtype=jnp.int32)[None, None, :])
    send_idx = jnp.sum(jnp.where(hit, jnp.arange(cubes_here, dtype=jnp.int32)[None, :, None], 0), axis=1)

    kv_rows = CAP * 2 * CUBE
    pooled = jnp.concatenate([local_k, local_v], axis=0)
    send_shape = jax.ShapeDtypeStruct((n_seq, kv_rows + 2 * cubes_here, HEAD_DIM), jnp.bfloat16)
    sends = pl.pallas_call(
        functools.partial(pack_kernel, cubes_here=cubes_here),
        out_shape=[send_shape] * heads_here,
        grid_spec=pltpu.PrefetchScalarGridSpec(
            num_scalar_prefetch=1,
            grid=(n_seq,),
            in_specs=[
                pl.BlockSpec((cubes_here, CUBE, feat), lambda b, t: (0, 0, 0)),
                pl.BlockSpec((cubes_here, CUBE, feat), lambda b, t: (0, 0, 0)),
                pl.BlockSpec((2 * cubes_here, feat), lambda b, t: (0, 0)),
            ],
            out_specs=[pl.BlockSpec((None, kv_rows + 2 * cubes_here, HEAD_DIM), lambda b, t: (b, 0, 0))]
            * heads_here,
        ),
    )(send_idx, k3, v3, pooled)
    recvs = [lax.all_to_all(x, "seq", 0, 0, tiled=True) for x in sends]

    rank_from = jnp.clip(jnp.cumsum(listed_me, axis=1) - 1, 0, CAP - 1)
    src = pattern // cubes_here
    loc = pattern % cubes_here
    own = src == me
    src_tbl = jnp.where(own, -1, src).astype(jnp.int32)
    row_tbl = jnp.where(own, loc, rank_from[src, loc] * (2 * CUBE)).astype(jnp.int32)

    okv = jnp.concatenate([k3, v3], axis=1)
    full2 = lambda i, a, r: (0, 0)
    hbm = pl.BlockSpec(memory_space=pl.ANY)
    outs = []
    for h, recv in enumerate(recvs):
        pooled_k = recv[:, kv_rows:kv_rows + cubes_here, :].reshape(n_cubes, HEAD_DIM)
        pooled_v = recv[:, kv_rows + cubes_here:, :].reshape(n_cubes, HEAD_DIM)
        outs.append(pl.pallas_call(
            functools.partial(attend_kernel, n_sel=n_sel, head=h),
            out_shape=jax.ShapeDtypeStruct((tok_rows, HEAD_DIM), jnp.bfloat16),
            grid_spec=pltpu.PrefetchScalarGridSpec(
                num_scalar_prefetch=2,
                grid=(cubes_here,),
                in_specs=[
                    pl.BlockSpec((CUBE, HEAD_DIM), lambda i, a, r, h=h: (i, h)),
                    hbm,
                    hbm,
                    pl.BlockSpec((n_cubes, HEAD_DIM), full2),
                    pl.BlockSpec((n_cubes, HEAD_DIM), full2),
                ],
                out_specs=pl.BlockSpec((CUBE, HEAD_DIM), lambda i, a, r: (i, 0)),
                scratch_shapes=[
                    pltpu.VMEM((2, n_sel, 2 * CUBE, HEAD_DIM), jnp.bfloat16),
                    pltpu.SemaphoreType.DMA((2,)),
                ],
            ),
            compiler_params=pltpu.CompilerParams(
                dimension_semantics=("arbitrary",), vmem_limit_bytes=32 * 1024 * 1024),
        )(src_tbl, row_tbl, queries, okv, recv, pooled_k, pooled_v))
    attended = jnp.concatenate(outs, axis=1)

    pair = ("yh", "core")
    n_pair = lax.psum(1, pair)
    n_x = lax.psum(1, "x")
    w_all = lax.all_gather(w_out, pair, axis=0, tiled=True)
    per_dest = attended.reshape(-1, n_x, 2, CUBE, feat)
    per_dest = jnp.transpose(per_dest, (0, 2, 1, 3, 4)).reshape(n_pair, n_x * CUBE, feat)
    got = lax.all_to_all(per_dest, pair, 0, 0, tiled=True)
    partial = None
    for g in range(n_pair):
        term = jnp.dot(got[g], w_all[g * feat:(g + 1) * feat], preferred_element_type=jnp.float32)
        term = term.astype(jnp.bfloat16).astype(jnp.float32)
        partial = term if partial is None else partial + term
    spread = lax.all_to_all(partial.astype(jnp.bfloat16).reshape(n_x, CUBE, -1), "x", 0, 0, tiled=True)
    summed = jnp.sum(spread.astype(jnp.float32), axis=0)
    return (summed * out_gate[None, :]).astype(jnp.bfloat16)


def solution(mesh):
    n_seq, n_head = mesh.devices.shape
    split = Mesh(mesh.devices.reshape(n_seq, 2, n_head // 4, 2), ("seq", "yh", "x", "core"))
    head = ("yh", "x", "core")
    return jax.shard_map(
        on_device,
        mesh=split,
        in_specs=(
            P("seq", head),
            P("seq", head),
            P("seq", head),
            P("seq", None),
            P(head, None),
            P(),
        ),
        out_specs=P(("seq", "yh", "x", "core"), None),
        check_vma=False,
    )
```

```python
import functools

import jax
import jax.numpy as jnp
from jax import lax
from jax.experimental import pallas as pl
from jax.experimental.pallas import tpu as pltpu
from jax.sharding import Mesh, PartitionSpec as P

HEAD_DIM = 128
CUBE = 64
CAP = 6


def attend_kernel(src_ref, row_ref, q_ref, okv_hbm, rv_hbm, pk_ref, pv_ref, o_ref,
                  kvbuf, sem, *, n_sel, heads_here, per_step):
    i = pl.program_id(0)
    steps = pl.num_programs(0)
    scale = HEAD_DIM ** (-0.5)

    def start(step, slot):
        for u in range(per_step):
            for j in range(n_sel):
                a = src_ref[step * per_step + u, j]
                r = row_ref[step * per_step + u, j]

                @pl.when(a < 0)
                def _():
                    pltpu.make_async_copy(okv_hbm.at[r], kvbuf.at[slot, u, j], sem.at[slot]).start()

                @pl.when(a >= 0)
                def _():
                    base = pl.multiple_of(r, 2 * CUBE)
                    pltpu.make_async_copy(
                        rv_hbm.at[a, pl.ds(base, 2 * CUBE)], kvbuf.at[slot, u, j], sem.at[slot]).start()

    @pl.when(i == 0)
    def _():
        start(0, 0)

    slot = i % 2

    @pl.when(i + 1 < steps)
    def _():
        start(i + 1, 1 - slot)

    pltpu.make_async_copy(kvbuf.at[slot], kvbuf.at[slot], sem.at[slot]).wait()

    def softmax_w(s):
        m = jnp.max(s, axis=-1, keepdims=True)
        p = jnp.exp(s - m)
        return (p / jnp.sum(p, axis=-1, keepdims=True)).astype(jnp.bfloat16)

    dims = (((1,), (1,)), ((), ()))
    for u in range(per_step):
        rows = pl.ds(u * CUBE, CUBE)
        for h in range(heads_here):
            cols = pl.ds(h * HEAD_DIM, HEAD_DIM)
            q = q_ref[rows, cols]
            k = kvbuf[slot, u, :, pl.ds(0, CUBE), cols].reshape(n_sel * CUBE, HEAD_DIM)
            v = kvbuf[slot, u, :, pl.ds(CUBE, CUBE), cols].reshape(n_sel * CUBE, HEAD_DIM)
            s_f = lax.dot_general(q, k, dims, preferred_element_type=jnp.float32) * scale
            fine = jnp.dot(softmax_w(s_f), v, preferred_element_type=jnp.float32)
            s_c = lax.dot_general(q, pk_ref[:, cols], dims, preferred_element_type=jnp.float32) * scale
            coarse = jnp.dot(softmax_w(s_c), pv_ref[:, cols], preferred_element_type=jnp.float32)
            o_ref[rows, cols] = (fine + coarse).astype(jnp.bfloat16)


def pack_kernel(idx_ref, k_ref, v_ref, pooled_ref, o_ref, *, cubes_here):
    b = pl.program_id(0)
    for r in range(CAP):
        c = idx_ref[b, r]
        o_ref[pl.ds(r * 2 * CUBE, CUBE), :] = k_ref[c]
        o_ref[pl.ds(r * 2 * CUBE + CUBE, CUBE), :] = v_ref[c]
    o_ref[pl.ds(CAP * 2 * CUBE, 2 * cubes_here), :] = pooled_ref[...]


def on_device(queries, key_tokens, value_tokens, pattern, w_out, out_gate):
    tok_rows, feat = queries.shape
    heads_here = feat // HEAD_DIM
    cubes_here = tok_rows // CUBE
    n_sel = pattern.shape[1]
    n_seq = lax.psum(1, "seq")
    me = lax.axis_index("seq")
    n_cubes = cubes_here * n_seq

    k3 = key_tokens.reshape(cubes_here, CUBE, feat)
    v3 = value_tokens.reshape(cubes_here, CUBE, feat)
    local_k = jnp.mean(k3.astype(jnp.float32), axis=1).astype(jnp.bfloat16)
    local_v = jnp.mean(v3.astype(jnp.float32), axis=1).astype(jnp.bfloat16)

    listed_me = jnp.any(
        pattern.reshape(-1)[:, None] == jnp.arange(n_cubes, dtype=jnp.int32)[None, :], axis=0
    ).astype(jnp.int32).reshape(n_seq, cubes_here)
    need_by = lax.all_to_all(listed_me, "seq", 0, 0, tiled=True) > 0
    pos_by = jnp.cumsum(need_by.astype(jnp.int32), axis=1) - 1
    hit = need_by[:, :, None] & (pos_by[:, :, None] == jnp.arange(CAP, dtype=jnp.int32)[None, None, :])
    send_idx = jnp.sum(jnp.where(hit, jnp.arange(cubes_here, dtype=jnp.int32)[None, :, None], 0), axis=1)

    kv_rows = CAP * 2 * CUBE
    pooled = jnp.concatenate([local_k, local_v], axis=0)
    send = pl.pallas_call(
        functools.partial(pack_kernel, cubes_here=cubes_here),
        out_shape=jax.ShapeDtypeStruct((n_seq, kv_rows + 2 * cubes_here, feat), jnp.bfloat16),
        grid_spec=pltpu.PrefetchScalarGridSpec(
            num_scalar_prefetch=1,
            grid=(n_seq,),
            in_specs=[
                pl.BlockSpec((cubes_here, CUBE, feat), lambda b, t: (0, 0, 0)),
                pl.BlockSpec((cubes_here, CUBE, feat), lambda b, t: (0, 0, 0)),
                pl.BlockSpec((2 * cubes_here, feat), lambda b, t: (0, 0)),
            ],
            out_specs=pl.BlockSpec((None, kv_rows + 2 * cubes_here, feat), lambda b, t: (b, 0, 0)),
        ),
    )(send_idx, k3, v3, pooled)
    recv = lax.all_to_all(send, "seq", 0, 0, tiled=True)

    pooled_k = recv[:, kv_rows:kv_rows + cubes_here, :].reshape(n_cubes, feat)
    pooled_v = recv[:, kv_rows + cubes_here:, :].reshape(n_cubes, feat)

    rank_from = jnp.clip(jnp.cumsum(listed_me, axis=1) - 1, 0, CAP - 1)
    src = pattern // cubes_here
    loc = pattern % cubes_here
    own = src == me
    src_tbl = jnp.where(own, -1, src).astype(jnp.int32)
    row_tbl = jnp.where(own, loc, rank_from[src, loc] * (2 * CUBE)).astype(jnp.int32)

    per_step = 2
    kern = functools.partial(attend_kernel, n_sel=n_sel, heads_here=heads_here, per_step=per_step)
    full2 = lambda i, a, r: (0, 0)
    hbm = pl.BlockSpec(memory_space=pl.ANY)
    attended = pl.pallas_call(
        kern,
        out_shape=jax.ShapeDtypeStruct((tok_rows, feat), jnp.bfloat16),
        grid_spec=pltpu.PrefetchScalarGridSpec(
            num_scalar_prefetch=2,
            grid=(cubes_here // per_step,),
            in_specs=[
                pl.BlockSpec((per_step * CUBE, feat), lambda i, a, r: (i, 0)),
                hbm,
                hbm,
                pl.BlockSpec((n_cubes, feat), full2),
                pl.BlockSpec((n_cubes, feat), full2),
            ],
            out_specs=pl.BlockSpec((per_step * CUBE, feat), lambda i, a, r: (i, 0)),
            scratch_shapes=[
                pltpu.VMEM((2, per_step, n_sel, 2 * CUBE, feat), jnp.bfloat16),
                pltpu.SemaphoreType.DMA((2,)),
            ],
        ),
        compiler_params=pltpu.CompilerParams(
            dimension_semantics=("arbitrary",), vmem_limit_bytes=32 * 1024 * 1024),
    )(src_tbl, row_tbl, queries, jnp.concatenate([k3, v3], axis=1), recv, pooled_k, pooled_v)

    pair = ("yh", "core")
    n_pair = lax.psum(1, pair)
    n_x = lax.psum(1, "x")
    w_all = lax.all_gather(w_out, pair, axis=0, tiled=True)
    per_dest = attended.reshape(-1, n_x, 2, CUBE, feat)
    per_dest = jnp.transpose(per_dest, (0, 2, 1, 3, 4)).reshape(n_pair, n_x * CUBE, feat)
    got = lax.all_to_all(per_dest, pair, 0, 0, tiled=True)
    partial = None
    for g in range(n_pair):
        term = jnp.dot(got[g], w_all[g * feat:(g + 1) * feat], preferred_element_type=jnp.float32)
        term = term.astype(jnp.bfloat16).astype(jnp.float32)
        partial = term if partial is None else partial + term
    spread = lax.all_to_all(partial.astype(jnp.bfloat16).reshape(n_x, CUBE, -1), "x", 0, 0, tiled=True)
    summed = jnp.sum(spread.astype(jnp.float32), axis=0)
    return (summed * out_gate[None, :]).astype(jnp.bfloat16)


def solution(mesh):
    n_seq, n_head = mesh.devices.shape
    split = Mesh(mesh.devices.reshape(n_seq, 2, n_head // 4, 2), ("seq", "yh", "x", "core"))
    head = ("yh", "x", "core")
    return jax.shard_map(
        on_device,
        mesh=split,
        in_specs=(
            P("seq", head),
            P("seq", head),
            P("seq", head),
            P("seq", None),
            P(head, None),
            P(),
        ),
        out_specs=P(("seq", "yh", "x", "core"), None),
        check_vma=False,
    )
```

```python
import functools

import jax
import jax.numpy as jnp
from jax import lax
from jax.experimental import pallas as pl
from jax.experimental.pallas import tpu as pltpu
from jax.sharding import Mesh, PartitionSpec as P

HEAD_DIM = 128
CUBE = 64
CAP = 6


def attend_kernel(src_ref, row_ref, q_ref, okv_hbm, rv_hbm, pk_ref, pv_ref, o_ref,
                  kvbuf, sem, *, n_sel, heads_here, per_step):
    i = pl.program_id(0)
    steps = pl.num_programs(0)
    scale = HEAD_DIM ** (-0.5)

    def start(step, slot):
        for u in range(per_step):
            for j in range(n_sel):
                a = src_ref[step * per_step + u, j]
                r = row_ref[step * per_step + u, j]

                @pl.when(a < 0)
                def _():
                    pltpu.make_async_copy(okv_hbm.at[r], kvbuf.at[slot, u, j], sem.at[slot]).start()

                @pl.when(a >= 0)
                def _():
                    base = pl.multiple_of(r, CUBE)
                    pltpu.make_async_copy(
                        rv_hbm.at[a, pl.ds(base, CUBE)], kvbuf.at[slot, u, j], sem.at[slot]).start()

    @pl.when(i == 0)
    def _():
        start(0, 0)

    slot = i % 2

    @pl.when(i + 1 < steps)
    def _():
        start(i + 1, 1 - slot)

    pltpu.make_async_copy(kvbuf.at[slot], kvbuf.at[slot], sem.at[slot]).wait()

    def softmax_w(s):
        m = jnp.max(s, axis=-1, keepdims=True)
        p = jnp.exp(s - m)
        return (p / jnp.sum(p, axis=-1, keepdims=True)).astype(jnp.bfloat16)

    dims = (((1,), (1,)), ((), ()))
    for u in range(per_step):
        rows = pl.ds(u * CUBE, CUBE)
        for h in range(heads_here):
            cols = pl.ds(h * HEAD_DIM, HEAD_DIM)
            q = q_ref[rows, cols]
            k = kvbuf[slot, u, :, :, cols].reshape(n_sel * CUBE, HEAD_DIM)
            v = kvbuf[slot, u, :, :, pl.ds(heads_here * HEAD_DIM + h * HEAD_DIM, HEAD_DIM)].reshape(
                n_sel * CUBE, HEAD_DIM)
            s_f = lax.dot_general(q, k, dims, preferred_element_type=jnp.float32) * scale
            fine = jnp.dot(softmax_w(s_f), v, preferred_element_type=jnp.float32)
            s_c = lax.dot_general(q, pk_ref[:, cols], dims, preferred_element_type=jnp.float32) * scale
            coarse = jnp.dot(softmax_w(s_c), pv_ref[:, cols], preferred_element_type=jnp.float32)
            o_ref[rows, cols] = (fine + coarse).astype(jnp.bfloat16)


def pack_kernel(idx_ref, kv_ref, pooled_ref, o_ref):
    b = pl.program_id(0)
    for r in range(CAP):
        o_ref[pl.ds(r * CUBE, CUBE), :] = kv_ref[idx_ref[b, r]]
    o_ref[pl.ds(CAP * CUBE, pooled_ref.shape[0]), :] = pooled_ref[...]


def on_device(queries, key_tokens, value_tokens, pattern, w_out, out_gate):
    tok_rows, feat = queries.shape
    heads_here = feat // HEAD_DIM
    cubes_here = tok_rows // CUBE
    n_sel = pattern.shape[1]
    n_seq = lax.psum(1, "seq")
    me = lax.axis_index("seq")
    n_cubes = cubes_here * n_seq

    k3 = key_tokens.reshape(cubes_here, CUBE, feat)
    v3 = value_tokens.reshape(cubes_here, CUBE, feat)
    local_k = jnp.mean(k3.astype(jnp.float32), axis=1).astype(jnp.bfloat16)
    local_v = jnp.mean(v3.astype(jnp.float32), axis=1).astype(jnp.bfloat16)

    listed_me = jnp.any(
        pattern.reshape(-1)[:, None] == jnp.arange(n_cubes, dtype=jnp.int32)[None, :], axis=0
    ).astype(jnp.int32).reshape(n_seq, cubes_here)
    need_by = lax.all_to_all(listed_me, "seq", 0, 0, tiled=True) > 0
    pos_by = jnp.cumsum(need_by.astype(jnp.int32), axis=1) - 1
    hit = need_by[:, :, None] & (pos_by[:, :, None] == jnp.arange(CAP, dtype=jnp.int32)[None, None, :])
    send_idx = jnp.sum(jnp.where(hit, jnp.arange(cubes_here, dtype=jnp.int32)[None, :, None], 0), axis=1)

    kv_rows = CAP * CUBE
    okv = jnp.concatenate([k3, v3], axis=2)
    pooled = jnp.concatenate([local_k, local_v], axis=1)
    send = pl.pallas_call(
        pack_kernel,
        out_shape=jax.ShapeDtypeStruct((n_seq, kv_rows + cubes_here, 2 * feat), jnp.bfloat16),
        grid_spec=pltpu.PrefetchScalarGridSpec(
            num_scalar_prefetch=1,
            grid=(n_seq,),
            in_specs=[
                pl.BlockSpec((cubes_here, CUBE, 2 * feat), lambda b, t: (0, 0, 0)),
                pl.BlockSpec((cubes_here, 2 * feat), lambda b, t: (0, 0)),
            ],
            out_specs=pl.BlockSpec((None, kv_rows + cubes_here, 2 * feat), lambda b, t: (b, 0, 0)),
        ),
    )(send_idx, okv, pooled)
    recv = lax.all_to_all(send, "seq", 0, 0, tiled=True)

    pooled_k = recv[:, kv_rows:, :feat].reshape(n_cubes, feat)
    pooled_v = recv[:, kv_rows:, feat:].reshape(n_cubes, feat)

    rank_from = jnp.clip(jnp.cumsum(listed_me, axis=1) - 1, 0, CAP - 1)
    src = pattern // cubes_here
    loc = pattern % cubes_here
    own = src == me
    src_tbl = jnp.where(own, -1, src).astype(jnp.int32)
    row_tbl = jnp.where(own, loc, rank_from[src, loc] * CUBE).astype(jnp.int32)

    per_step = 2
    kern = functools.partial(attend_kernel, n_sel=n_sel, heads_here=heads_here, per_step=per_step)
    full2 = lambda i, a, r: (0, 0)
    hbm = pl.BlockSpec(memory_space=pl.ANY)
    attended = pl.pallas_call(
        kern,
        out_shape=jax.ShapeDtypeStruct((tok_rows, feat), jnp.bfloat16),
        grid_spec=pltpu.PrefetchScalarGridSpec(
            num_scalar_prefetch=2,
            grid=(cubes_here // per_step,),
            in_specs=[
                pl.BlockSpec((per_step * CUBE, feat), lambda i, a, r: (i, 0)),
                hbm,
                hbm,
                pl.BlockSpec((n_cubes, feat), full2),
                pl.BlockSpec((n_cubes, feat), full2),
            ],
            out_specs=pl.BlockSpec((per_step * CUBE, feat), lambda i, a, r: (i, 0)),
            scratch_shapes=[
                pltpu.VMEM((2, per_step, n_sel, CUBE, 2 * feat), jnp.bfloat16),
                pltpu.SemaphoreType.DMA((2,)),
            ],
        ),
        compiler_params=pltpu.CompilerParams(
            dimension_semantics=("arbitrary",), vmem_limit_bytes=32 * 1024 * 1024),
    )(src_tbl, row_tbl, queries, okv, recv, pooled_k, pooled_v)

    pair = ("yh", "core")
    n_pair = lax.psum(1, pair)
    n_x = lax.psum(1, "x")
    w_all = lax.all_gather(w_out, pair, axis=0, tiled=True)
    per_dest = attended.reshape(-1, n_x, 2, CUBE, feat)
    per_dest = jnp.transpose(per_dest, (0, 2, 1, 3, 4)).reshape(n_pair, n_x * CUBE, feat)
    got = lax.all_to_all(per_dest, pair, 0, 0, tiled=True)
    partial = None
    for g in range(n_pair):
        term = jnp.dot(got[g], w_all[g * feat:(g + 1) * feat], preferred_element_type=jnp.float32)
        term = term.astype(jnp.bfloat16).astype(jnp.float32)
        partial = term if partial is None else partial + term
    spread = lax.all_to_all(partial.astype(jnp.bfloat16).reshape(n_x, CUBE, -1), "x", 0, 0, tiled=True)
    summed = jnp.sum(spread.astype(jnp.float32), axis=0)
    return (summed * out_gate[None, :]).astype(jnp.bfloat16)


def solution(mesh):
    n_seq, n_head = mesh.devices.shape
    split = Mesh(mesh.devices.reshape(n_seq, 2, n_head // 4, 2), ("seq", "yh", "x", "core"))
    head = ("yh", "x", "core")
    return jax.shard_map(
        on_device,
        mesh=split,
        in_specs=(
            P("seq", head),
            P("seq", head),
            P("seq", head),
            P("seq", None),
            P(head, None),
            P(),
        ),
        out_specs=P(("seq", "yh", "x", "core"), None),
        check_vma=False,
    )
```

```python
import functools

import jax
import jax.numpy as jnp
from jax import lax
from jax.experimental import pallas as pl
from jax.experimental.pallas import tpu as pltpu
from jax.sharding import Mesh, PartitionSpec as P

HEAD_DIM = 128
CUBE = 64
CAP = 6


def attend_kernel(row_ref, q_ref, cand_hbm, pk_ref, pv_ref, o_ref,
                  kvbuf, sem, *, n_sel, heads_here, per_step):
    i = pl.program_id(0)
    steps = pl.num_programs(0)
    scale = HEAD_DIM ** (-0.5)

    def start(step, slot):
        for u in range(per_step):
            for j in range(n_sel):
                base = pl.multiple_of(row_ref[step * per_step + u, j], CUBE)
                pltpu.make_async_copy(
                    cand_hbm.at[pl.ds(base, CUBE)], kvbuf.at[slot, u, j], sem.at[slot]).start()

    @pl.when(i == 0)
    def _():
        start(0, 0)

    slot = i % 2

    @pl.when(i + 1 < steps)
    def _():
        start(i + 1, 1 - slot)

    pltpu.make_async_copy(kvbuf.at[slot], kvbuf.at[slot], sem.at[slot]).wait()

    def softmax_w(s):
        m = jnp.max(s, axis=-1, keepdims=True)
        p = jnp.exp(s - m)
        return (p / jnp.sum(p, axis=-1, keepdims=True)).astype(jnp.bfloat16)

    dims = (((1,), (1,)), ((), ()))
    for u in range(per_step):
        rows = pl.ds(u * CUBE, CUBE)
        for h in range(heads_here):
            cols = pl.ds(h * HEAD_DIM, HEAD_DIM)
            q = q_ref[rows, cols]
            k = kvbuf[slot, u, :, :, cols].reshape(n_sel * CUBE, HEAD_DIM)
            v = kvbuf[slot, u, :, :, pl.ds(heads_here * HEAD_DIM + h * HEAD_DIM, HEAD_DIM)].reshape(
                n_sel * CUBE, HEAD_DIM)
            s_f = lax.dot_general(q, k, dims, preferred_element_type=jnp.float32) * scale
            fine = jnp.dot(softmax_w(s_f), v, preferred_element_type=jnp.float32)
            s_c = lax.dot_general(q, pk_ref[:, cols], dims, preferred_element_type=jnp.float32) * scale
            coarse = jnp.dot(softmax_w(s_c), pv_ref[:, cols], preferred_element_type=jnp.float32)
            o_ref[rows, cols] = (fine + coarse).astype(jnp.bfloat16)


def pack_kernel(idx_ref, kv_ref, pooled_ref, o_ref):
    b = pl.program_id(0)
    for r in range(CAP):
        o_ref[pl.ds(r * CUBE, CUBE), :] = kv_ref[idx_ref[b, r]]
    o_ref[pl.ds(CAP * CUBE, pooled_ref.shape[0]), :] = pooled_ref[...]


def on_device(queries, key_tokens, value_tokens, pattern, w_out, out_gate):
    tok_rows, feat = queries.shape
    heads_here = feat // HEAD_DIM
    cubes_here = tok_rows // CUBE
    n_sel = pattern.shape[1]
    n_seq = lax.psum(1, "seq")
    me = lax.axis_index("seq")
    n_cubes = cubes_here * n_seq

    k3 = key_tokens.reshape(cubes_here, CUBE, feat)
    v3 = value_tokens.reshape(cubes_here, CUBE, feat)
    local_k = jnp.mean(k3.astype(jnp.float32), axis=1).astype(jnp.bfloat16)
    local_v = jnp.mean(v3.astype(jnp.float32), axis=1).astype(jnp.bfloat16)

    listed_me = jnp.any(
        pattern.reshape(-1)[:, None] == jnp.arange(n_cubes, dtype=jnp.int32)[None, :], axis=0
    ).astype(jnp.int32).reshape(n_seq, cubes_here)
    need_by = lax.all_to_all(listed_me, "seq", 0, 0, tiled=True) > 0
    pos_by = jnp.cumsum(need_by.astype(jnp.int32), axis=1) - 1
    hit = need_by[:, :, None] & (pos_by[:, :, None] == jnp.arange(CAP, dtype=jnp.int32)[None, None, :])
    send_idx = jnp.sum(jnp.where(hit, jnp.arange(cubes_here, dtype=jnp.int32)[None, :, None], 0), axis=1)

    kv_rows = CAP * CUBE
    okv = jnp.concatenate([k3, v3], axis=2)
    pooled = jnp.concatenate([local_k, local_v], axis=1)
    send = pl.pallas_call(
        pack_kernel,
        out_shape=jax.ShapeDtypeStruct((n_seq, kv_rows + cubes_here, 2 * feat), jnp.bfloat16),
        grid_spec=pltpu.PrefetchScalarGridSpec(
            num_scalar_prefetch=1,
            grid=(n_seq,),
            in_specs=[
                pl.BlockSpec((cubes_here, CUBE, 2 * feat), lambda b, t: (0, 0, 0)),
                pl.BlockSpec((cubes_here, 2 * feat), lambda b, t: (0, 0)),
            ],
            out_specs=pl.BlockSpec((None, kv_rows + cubes_here, 2 * feat), lambda b, t: (b, 0, 0)),
        ),
    )(send_idx, okv, pooled)
    recv = lax.all_to_all(send, "seq", 0, 0, tiled=True)

    pooled_k = recv[:, kv_rows:, :feat].reshape(n_cubes, feat)
    pooled_v = recv[:, kv_rows:, feat:].reshape(n_cubes, feat)

    rank_from = jnp.clip(jnp.cumsum(listed_me, axis=1) - 1, 0, CAP - 1)
    src = pattern // cubes_here
    loc = pattern % cubes_here
    own = src == me
    chunk = recv.shape[1]
    row_tbl = jnp.where(
        own, loc * CUBE, cubes_here * CUBE + src * chunk + rank_from[src, loc] * CUBE
    ).astype(jnp.int32)
    cand = jnp.concatenate([okv.reshape(-1, 2 * feat), recv.reshape(-1, 2 * feat)], axis=0)

    per_step = 2
    kern = functools.partial(attend_kernel, n_sel=n_sel, heads_here=heads_here, per_step=per_step)
    full2 = lambda i, r: (0, 0)
    hbm = pl.BlockSpec(memory_space=pl.ANY)
    attended = pl.pallas_call(
        kern,
        out_shape=jax.ShapeDtypeStruct((tok_rows, feat), jnp.bfloat16),
        grid_spec=pltpu.PrefetchScalarGridSpec(
            num_scalar_prefetch=1,
            grid=(cubes_here // per_step,),
            in_specs=[
                pl.BlockSpec((per_step * CUBE, feat), lambda i, r: (i, 0)),
                hbm,
                pl.BlockSpec((n_cubes, feat), full2),
                pl.BlockSpec((n_cubes, feat), full2),
            ],
            out_specs=pl.BlockSpec((per_step * CUBE, feat), lambda i, r: (i, 0)),
            scratch_shapes=[
                pltpu.VMEM((2, per_step, n_sel, CUBE, 2 * feat), jnp.bfloat16),
                pltpu.SemaphoreType.DMA((2,)),
            ],
        ),
        compiler_params=pltpu.CompilerParams(
            dimension_semantics=("arbitrary",), vmem_limit_bytes=32 * 1024 * 1024),
    )(row_tbl, queries, cand, pooled_k, pooled_v)

    pair = ("yh", "core")
    n_pair = lax.psum(1, pair)
    n_x = lax.psum(1, "x")
    w_all = lax.all_gather(w_out, pair, axis=0, tiled=True)
    per_dest = attended.reshape(-1, n_x, 2, CUBE, feat)
    per_dest = jnp.transpose(per_dest, (0, 2, 1, 3, 4)).reshape(n_pair, n_x * CUBE, feat)
    got = lax.all_to_all(per_dest, pair, 0, 0, tiled=True)
    partial = None
    for g in range(n_pair):
        term = jnp.dot(got[g], w_all[g * feat:(g + 1) * feat], preferred_element_type=jnp.float32)
        term = term.astype(jnp.bfloat16).astype(jnp.float32)
        partial = term if partial is None else partial + term
    spread = lax.all_to_all(partial.astype(jnp.bfloat16).reshape(n_x, CUBE, -1), "x", 0, 0, tiled=True)
    summed = jnp.sum(spread.astype(jnp.float32), axis=0)
    return (summed * out_gate[None, :]).astype(jnp.bfloat16)


def solution(mesh):
    n_seq, n_head = mesh.devices.shape
    split = Mesh(mesh.devices.reshape(n_seq, 2, n_head // 4, 2), ("seq", "yh", "x", "core"))
    head = ("yh", "x", "core")
    return jax.shard_map(
        on_device,
        mesh=split,
        in_specs=(
            P("seq", head),
            P("seq", head),
            P("seq", head),
            P("seq", None),
            P(head, None),
            P(),
        ),
        out_specs=P(("seq", "yh", "x", "core"), None),
        check_vma=False,
    )
```

```python
import functools

import jax
import jax.numpy as jnp
from jax import lax
from jax.experimental import pallas as pl
from jax.experimental.pallas import tpu as pltpu
from jax.sharding import Mesh, PartitionSpec as P

HEAD_DIM = 128
CUBE = 64
CAP = 6


def attend_kernel(src_ref, row_ref, q_ref, okv_hbm, rv_hbm, pk_ref, pv_ref, o_ref,
                  kvbuf, sem, *, n_sel, heads_here, per_step):
    i = pl.program_id(0)
    steps = pl.num_programs(0)
    scale = HEAD_DIM ** (-0.5)

    def start(step, slot):
        for u in range(per_step):
            for j in range(n_sel):
                a = src_ref[step * per_step + u, j]
                r = row_ref[step * per_step + u, j]

                @pl.when(a < 0)
                def _():
                    pltpu.make_async_copy(okv_hbm.at[r], kvbuf.at[slot, u, j], sem.at[slot]).start()

                @pl.when(a >= 0)
                def _():
                    base = pl.multiple_of(r, CUBE)
                    pltpu.make_async_copy(
                        rv_hbm.at[a, pl.ds(base, CUBE)], kvbuf.at[slot, u, j], sem.at[slot]).start()

    @pl.when(i == 0)
    def _():
        start(0, 0)

    slot = i % 2

    @pl.when(i + 1 < steps)
    def _():
        start(i + 1, 1 - slot)

    pltpu.make_async_copy(kvbuf.at[slot], kvbuf.at[slot], sem.at[slot]).wait()

    def softmax_w(s):
        m = jnp.max(s, axis=-1, keepdims=True)
        p = jnp.exp(s - m)
        return (p / jnp.sum(p, axis=-1, keepdims=True)).astype(jnp.bfloat16)

    dims = (((1,), (1,)), ((), ()))
    for u in range(per_step):
        rows = pl.ds(u * CUBE, CUBE)
        for h in range(heads_here):
            cols = pl.ds(h * HEAD_DIM, HEAD_DIM)
            q = q_ref[rows, cols]
            k = kvbuf[slot, u, :, :, cols].reshape(n_sel * CUBE, HEAD_DIM)
            v = kvbuf[slot, u, :, :, pl.ds(heads_here * HEAD_DIM + h * HEAD_DIM, HEAD_DIM)].reshape(
                n_sel * CUBE, HEAD_DIM)
            s_f = lax.dot_general(q, k, dims, preferred_element_type=jnp.float32) * scale
            fine = jnp.dot(softmax_w(s_f), v, preferred_element_type=jnp.float32)
            s_c = lax.dot_general(q, pk_ref[:, cols], dims, preferred_element_type=jnp.float32) * scale
            coarse = jnp.dot(softmax_w(s_c), pv_ref[:, cols], preferred_element_type=jnp.float32)
            o_ref[rows, cols] = (fine + coarse).astype(jnp.bfloat16)


def pack_kernel(idx_ref, kv_ref, pooled_ref, o_ref):
    b = pl.program_id(0)
    for r in range(CAP):
        o_ref[pl.ds(r * CUBE, CUBE), :] = kv_ref[idx_ref[b, r]]
    o_ref[pl.ds(CAP * CUBE, pooled_ref.shape[0]), :] = pooled_ref[...]


def on_device(queries, key_tokens, value_tokens, pattern, w_out, out_gate):
    tok_rows, feat = queries.shape
    heads_here = feat // HEAD_DIM
    cubes_here = tok_rows // CUBE
    n_sel = pattern.shape[1]
    n_seq = lax.psum(1, "seq")
    me = lax.axis_index("seq")
    n_cubes = cubes_here * n_seq

    k3 = key_tokens.reshape(cubes_here, CUBE, feat)
    v3 = value_tokens.reshape(cubes_here, CUBE, feat)
    local_k = jnp.mean(k3.astype(jnp.float32), axis=1).astype(jnp.bfloat16)
    local_v = jnp.mean(v3.astype(jnp.float32), axis=1).astype(jnp.bfloat16)

    listed_me = jnp.any(
        pattern.reshape(-1)[:, None] == jnp.arange(n_cubes, dtype=jnp.int32)[None, :], axis=0
    ).astype(jnp.int32).reshape(n_seq, cubes_here)
    need_by = lax.all_to_all(listed_me, "seq", 0, 0, tiled=True) > 0
    pos_by = jnp.cumsum(need_by.astype(jnp.int32), axis=1) - 1
    hit = need_by[:, :, None] & (pos_by[:, :, None] == jnp.arange(CAP, dtype=jnp.int32)[None, None, :])
    send_idx = jnp.sum(jnp.where(hit, jnp.arange(cubes_here, dtype=jnp.int32)[None, :, None], 0), axis=1)

    kv_rows = CAP * CUBE
    okv = jnp.concatenate([k3, v3], axis=2)
    pooled = jnp.concatenate([local_k, local_v], axis=1)
    send = pl.pallas_call(
        pack_kernel,
        out_shape=jax.ShapeDtypeStruct((n_seq, kv_rows + cubes_here, 2 * feat), jnp.bfloat16),
        grid_spec=pltpu.PrefetchScalarGridSpec(
            num_scalar_prefetch=1,
            grid=(n_seq,),
            in_specs=[
                pl.BlockSpec((cubes_here, CUBE, 2 * feat), lambda b, t: (0, 0, 0)),
                pl.BlockSpec((cubes_here, 2 * feat), lambda b, t: (0, 0)),
            ],
            out_specs=pl.BlockSpec((None, kv_rows + cubes_here, 2 * feat), lambda b, t: (b, 0, 0)),
        ),
    )(send_idx, okv, pooled)
    recv = lax.all_to_all(send, "seq", 0, 0, tiled=True)

    pooled_k = recv[:, kv_rows:, :feat].reshape(n_cubes, feat)
    pooled_v = recv[:, kv_rows:, feat:].reshape(n_cubes, feat)

    rank_from = jnp.clip(jnp.cumsum(listed_me, axis=1) - 1, 0, CAP - 1)
    src = pattern // cubes_here
    loc = pattern % cubes_here
    own = src == me
    src_tbl = jnp.where(own, -1, src).astype(jnp.int32)
    row_tbl = jnp.where(own, loc, rank_from[src, loc] * CUBE).astype(jnp.int32)

    per_step = 2
    kern = functools.partial(attend_kernel, n_sel=n_sel, heads_here=heads_here, per_step=per_step)
    full2 = lambda i, a, r: (0, 0)
    hbm = pl.BlockSpec(memory_space=pl.ANY)
    attended = pl.pallas_call(
        kern,
        out_shape=jax.ShapeDtypeStruct((tok_rows, feat), jnp.bfloat16),
        grid_spec=pltpu.PrefetchScalarGridSpec(
            num_scalar_prefetch=2,
            grid=(cubes_here // per_step,),
            in_specs=[
                pl.BlockSpec((per_step * CUBE, feat), lambda i, a, r: (i, 0)),
                hbm,
                hbm,
                pl.BlockSpec((n_cubes, feat), full2),
                pl.BlockSpec((n_cubes, feat), full2),
            ],
            out_specs=pl.BlockSpec((per_step * CUBE, feat), lambda i, a, r: (i, 0)),
            scratch_shapes=[
                pltpu.VMEM((2, per_step, n_sel, CUBE, 2 * feat), jnp.bfloat16),
                pltpu.SemaphoreType.DMA((2,)),
            ],
        ),
        compiler_params=pltpu.CompilerParams(
            dimension_semantics=("arbitrary",), vmem_limit_bytes=32 * 1024 * 1024),
    )(src_tbl, row_tbl, queries, okv, recv, pooled_k, pooled_v)

    pair = ("yh", "core")
    n_pair = lax.psum(1, pair)
    n_x = lax.psum(1, "x")
    w_all = lax.all_gather(w_out, pair, axis=0, tiled=True)
    per_dest = attended.reshape(-1, n_x, 2, CUBE, feat)
    per_dest = jnp.transpose(per_dest, (0, 2, 1, 3, 4)).reshape(n_pair, n_x * CUBE, feat)
    me_pair = lax.axis_index(pair)
    partial = None
    for k in range(n_pair):
        if k == 0:
            got = lax.dynamic_index_in_dim(per_dest, me_pair, axis=0, keepdims=False)
        else:
            out = lax.dynamic_index_in_dim(per_dest, me_pair ^ k, axis=0, keepdims=False)
            got = lax.ppermute(out, pair, [(g, g ^ k) for g in range(n_pair)])
        rows = lax.dynamic_slice_in_dim(w_all, (me_pair ^ k) * feat, feat, axis=0)
        term = jnp.dot(got, rows, preferred_element_type=jnp.float32)
        term = term.astype(jnp.bfloat16).astype(jnp.float32)
        partial = term if partial is None else partial + term
    spread = lax.all_to_all(partial.astype(jnp.bfloat16).reshape(n_x, CUBE, -1), "x", 0, 0, tiled=True)
    summed = jnp.sum(spread.astype(jnp.float32), axis=0)
    return (summed * out_gate[None, :]).astype(jnp.bfloat16)


def solution(mesh):
    n_seq, n_head = mesh.devices.shape
    split = Mesh(mesh.devices.reshape(n_seq, 2, n_head // 4, 2), ("seq", "yh", "x", "core"))
    head = ("yh", "x", "core")
    return jax.shard_map(
        on_device,
        mesh=split,
        in_specs=(
            P("seq", head),
            P("seq", head),
            P("seq", head),
            P("seq", None),
            P(head, None),
            P(),
        ),
        out_specs=P(("seq", "yh", "x", "core"), None),
        check_vma=False,
    )
```

```python
import functools

import jax
import jax.numpy as jnp
from jax import lax
from jax.experimental import pallas as pl
from jax.experimental.pallas import tpu as pltpu
from jax.sharding import Mesh, PartitionSpec as P

HEAD_DIM = 128
CUBE = 64
CAP = 6


def attend_kernel(src_ref, row_ref, q_ref, okv_hbm, rv_hbm, pk_ref, pv_ref, o_ref,
                  kvbuf, sem, *, n_sel, heads_here, per_step):
    i = pl.program_id(0)
    steps = pl.num_programs(0)
    scale = HEAD_DIM ** (-0.5)

    def start(step, slot):
        for u in range(per_step):
            for j in range(n_sel):
                a = src_ref[step * per_step + u, j]
                r = row_ref[step * per_step + u, j]

                @pl.when(a < 0)
                def _():
                    pltpu.make_async_copy(okv_hbm.at[r], kvbuf.at[slot, u, j], sem.at[slot]).start()

                @pl.when(a >= 0)
                def _():
                    base = pl.multiple_of(r, CUBE)
                    pltpu.make_async_copy(
                        rv_hbm.at[a, pl.ds(base, CUBE)], kvbuf.at[slot, u, j], sem.at[slot]).start()

    @pl.when(i == 0)
    def _():
        start(0, 0)

    slot = i % 2

    @pl.when(i + 1 < steps)
    def _():
        start(i + 1, 1 - slot)

    pltpu.make_async_copy(kvbuf.at[slot], kvbuf.at[slot], sem.at[slot]).wait()

    def softmax_w(s):
        m = jnp.max(s, axis=-1, keepdims=True)
        p = jnp.exp(s - m)
        return (p / jnp.sum(p, axis=-1, keepdims=True)).astype(jnp.bfloat16)

    dims = (((1,), (1,)), ((), ()))
    for u in range(per_step):
        rows = pl.ds(u * CUBE, CUBE)
        for h in range(heads_here):
            cols = pl.ds(h * HEAD_DIM, HEAD_DIM)
            q = q_ref[rows, cols]
            k = kvbuf[slot, u, :, :, cols].reshape(n_sel * CUBE, HEAD_DIM)
            v = kvbuf[slot, u, :, :, pl.ds(heads_here * HEAD_DIM + h * HEAD_DIM, HEAD_DIM)].reshape(
                n_sel * CUBE, HEAD_DIM)
            s_f = lax.dot_general(q, k, dims, preferred_element_type=jnp.float32) * scale
            fine = jnp.dot(softmax_w(s_f), v, preferred_element_type=jnp.float32)
            s_c = lax.dot_general(q, pk_ref[:, cols], dims, preferred_element_type=jnp.float32) * scale
            coarse = jnp.dot(softmax_w(s_c), pv_ref[:, cols], preferred_element_type=jnp.float32)
            o_ref[rows, cols] = (fine + coarse).astype(jnp.bfloat16)


def pack_kernel(idx_ref, kv_ref, pooled_ref, o_ref):
    b = pl.program_id(0)
    for r in range(CAP):
        o_ref[pl.ds(r * CUBE, CUBE), :] = kv_ref[idx_ref[b, r]]
    o_ref[pl.ds(CAP * CUBE, pooled_ref.shape[0]), :] = pooled_ref[...]


def on_device(queries, key_tokens, value_tokens, pattern, w_out, out_gate):
    tok_rows, feat = queries.shape
    heads_here = feat // HEAD_DIM
    cubes_here = tok_rows // CUBE
    n_sel = pattern.shape[1]
    n_seq = lax.psum(1, "seq")
    me = lax.axis_index("seq")
    n_cubes = cubes_here * n_seq

    k3 = key_tokens.reshape(cubes_here, CUBE, feat)
    v3 = value_tokens.reshape(cubes_here, CUBE, feat)
    local_k = jnp.mean(k3.astype(jnp.float32), axis=1).astype(jnp.bfloat16)
    local_v = jnp.mean(v3.astype(jnp.float32), axis=1).astype(jnp.bfloat16)

    listed_me = jnp.any(
        pattern.reshape(-1)[:, None] == jnp.arange(n_cubes, dtype=jnp.int32)[None, :], axis=0
    ).astype(jnp.int32).reshape(n_seq, cubes_here)
    need_by = lax.all_to_all(listed_me, "seq", 0, 0, tiled=True) > 0
    pos_by = jnp.cumsum(need_by.astype(jnp.int32), axis=1) - 1
    hit = need_by[:, :, None] & (pos_by[:, :, None] == jnp.arange(CAP, dtype=jnp.int32)[None, None, :])
    send_idx = jnp.sum(jnp.where(hit, jnp.arange(cubes_here, dtype=jnp.int32)[None, :, None], 0), axis=1)

    kv_rows = CAP * CUBE
    okv = jnp.concatenate([k3, v3], axis=2)
    pooled = jnp.concatenate([local_k, local_v], axis=1)
    send = pl.pallas_call(
        pack_kernel,
        out_shape=jax.ShapeDtypeStruct((n_seq, kv_rows + cubes_here, 2 * feat), jnp.bfloat16),
        grid_spec=pltpu.PrefetchScalarGridSpec(
            num_scalar_prefetch=1,
            grid=(n_seq,),
            in_specs=[
                pl.BlockSpec((cubes_here, CUBE, 2 * feat), lambda b, t: (0, 0, 0)),
                pl.BlockSpec((cubes_here, 2 * feat), lambda b, t: (0, 0)),
            ],
            out_specs=pl.BlockSpec((None, kv_rows + cubes_here, 2 * feat), lambda b, t: (b, 0, 0)),
        ),
    )(send_idx, okv, pooled)
    recv = lax.all_to_all(send, "seq", 0, 0, tiled=True)

    pooled_k = recv[:, kv_rows:, :feat].reshape(n_cubes, feat)
    pooled_v = recv[:, kv_rows:, feat:].reshape(n_cubes, feat)

    rank_from = jnp.clip(jnp.cumsum(listed_me, axis=1) - 1, 0, CAP - 1)
    src = pattern // cubes_here
    loc = pattern % cubes_here
    own = src == me
    src_tbl = jnp.where(own, -1, src).astype(jnp.int32)
    row_tbl = jnp.where(own, loc, rank_from[src, loc] * CUBE).astype(jnp.int32)

    per_step = 2
    kern = functools.partial(attend_kernel, n_sel=n_sel, heads_here=heads_here, per_step=per_step)
    full2 = lambda i, a, r: (0, 0)
    hbm = pl.BlockSpec(memory_space=pl.ANY)
    attended = pl.pallas_call(
        kern,
        out_shape=jax.ShapeDtypeStruct((tok_rows, feat), jnp.bfloat16),
        grid_spec=pltpu.PrefetchScalarGridSpec(
            num_scalar_prefetch=2,
            grid=(cubes_here // per_step,),
            in_specs=[
                pl.BlockSpec((per_step * CUBE, feat), lambda i, a, r: (i, 0)),
                hbm,
                hbm,
                pl.BlockSpec((n_cubes, feat), full2),
                pl.BlockSpec((n_cubes, feat), full2),
            ],
            out_specs=pl.BlockSpec((per_step * CUBE, feat), lambda i, a, r: (i, 0)),
            scratch_shapes=[
                pltpu.VMEM((2, per_step, n_sel, CUBE, 2 * feat), jnp.bfloat16),
                pltpu.SemaphoreType.DMA((2,)),
            ],
        ),
        compiler_params=pltpu.CompilerParams(
            dimension_semantics=("arbitrary",), vmem_limit_bytes=32 * 1024 * 1024),
    )(src_tbl, row_tbl, queries, okv, recv, pooled_k, pooled_v)

    pair = ("yh", "core")
    n_pair = lax.psum(1, pair)
    n_x = lax.psum(1, "x")
    w_all = lax.all_gather(w_out, pair, axis=0, tiled=True)
    per_dest = attended.reshape(-1, n_x, 2, CUBE, feat)
    per_dest = jnp.transpose(per_dest, (0, 2, 1, 3, 4)).reshape(n_pair, n_x * CUBE, feat)
    me_pair = lax.axis_index(pair)
    partial = None
    for k in range(n_pair):
        if k == 0:
            got = lax.dynamic_index_in_dim(per_dest, me_pair, axis=0, keepdims=False)
        else:
            out = lax.dynamic_index_in_dim(per_dest, me_pair ^ k, axis=0, keepdims=False)
            got = lax.ppermute(out, pair, [(g, g ^ k) for g in range(n_pair)])
        rows = lax.dynamic_slice_in_dim(w_all, (me_pair ^ k) * feat, feat, axis=0)
        term = jnp.dot(got, rows, preferred_element_type=jnp.float32)
        term = term.astype(jnp.bfloat16).astype(jnp.float32)
        partial = term if partial is None else partial + term
    blocks = partial.astype(jnp.bfloat16).reshape(n_x, CUBE, -1)
    me_x = lax.axis_index("x")
    summed = lax.dynamic_index_in_dim(blocks, me_x, axis=0, keepdims=False).astype(jnp.float32)
    for k in range(1, n_x):
        out = lax.dynamic_index_in_dim(blocks, (me_x + k) % n_x, axis=0, keepdims=False)
        got = lax.ppermute(out, "x", [(g, (g + k) % n_x) for g in range(n_x)])
        summed = summed + got.astype(jnp.float32)
    return (summed * out_gate[None, :]).astype(jnp.bfloat16)


def solution(mesh):
    n_seq, n_head = mesh.devices.shape
    split = Mesh(mesh.devices.reshape(n_seq, 2, n_head // 4, 2), ("seq", "yh", "x", "core"))
    head = ("yh", "x", "core")
    return jax.shard_map(
        on_device,
        mesh=split,
        in_specs=(
            P("seq", head),
            P("seq", head),
            P("seq", head),
            P("seq", None),
            P(head, None),
            P(),
        ),
        out_specs=P(("seq", "yh", "x", "core"), None),
        check_vma=False,
    )
```

```python
import functools

import jax
import jax.numpy as jnp
from jax import lax
from jax.experimental import pallas as pl
from jax.experimental.pallas import tpu as pltpu
from jax.sharding import Mesh, PartitionSpec as P

HEAD_DIM = 128
CUBE = 64
CAP = 6


def attend_kernel(src_ref, row_ref, q_ref, okv_hbm, rv_hbm, pk_ref, pv_ref, o_ref,
                  kvbuf, sem, *, n_sel, heads_here, per_step):
    i = pl.program_id(0)
    steps = pl.num_programs(0)
    scale = HEAD_DIM ** (-0.5)

    def start(step, slot):
        for u in range(per_step):
            for j in range(n_sel):
                a = src_ref[step * per_step + u, j]
                r = row_ref[step * per_step + u, j]

                @pl.when(a < 0)
                def _():
                    pltpu.make_async_copy(okv_hbm.at[r], kvbuf.at[slot, u, j], sem.at[slot]).start()

                @pl.when(a >= 0)
                def _():
                    base = pl.multiple_of(r, CUBE)
                    pltpu.make_async_copy(
                        rv_hbm.at[a, pl.ds(base, CUBE)], kvbuf.at[slot, u, j], sem.at[slot]).start()

    @pl.when(i == 0)
    def _():
        start(0, 0)

    slot = i % 2

    @pl.when(i + 1 < steps)
    def _():
        start(i + 1, 1 - slot)

    pltpu.make_async_copy(kvbuf.at[slot], kvbuf.at[slot], sem.at[slot]).wait()

    def softmax_w(s):
        m = jnp.max(s, axis=-1, keepdims=True)
        p = jnp.exp(s - m)
        return (p / jnp.sum(p, axis=-1, keepdims=True)).astype(jnp.bfloat16)

    dims = (((1,), (1,)), ((), ()))
    for u in range(per_step):
        rows = pl.ds(u * CUBE, CUBE)
        for h in range(heads_here):
            cols = pl.ds(h * HEAD_DIM, HEAD_DIM)
            q = q_ref[rows, cols]
            k = kvbuf[slot, u, :, :, cols].reshape(n_sel * CUBE, HEAD_DIM)
            v = kvbuf[slot, u, :, :, pl.ds(heads_here * HEAD_DIM + h * HEAD_DIM, HEAD_DIM)].reshape(
                n_sel * CUBE, HEAD_DIM)
            s_f = lax.dot_general(q, k, dims, preferred_element_type=jnp.float32) * scale
            fine = jnp.dot(softmax_w(s_f), v, preferred_element_type=jnp.float32)
            s_c = lax.dot_general(q, pk_ref[:, cols], dims, preferred_element_type=jnp.float32) * scale
            coarse = jnp.dot(softmax_w(s_c), pv_ref[:, cols], preferred_element_type=jnp.float32)
            o_ref[rows, cols] = (fine + coarse).astype(jnp.bfloat16)


def pack_kernel(idx_ref, kv_ref, pooled_ref, o_ref):
    b = pl.program_id(0)
    for r in range(CAP):
        o_ref[pl.ds(r * CUBE, CUBE), :] = kv_ref[idx_ref[b, r]]
    o_ref[pl.ds(CAP * CUBE, pooled_ref.shape[0]), :] = pooled_ref[...]


def on_device(queries, key_tokens, value_tokens, pattern, w_out, out_gate):
    tok_rows, feat = queries.shape
    heads_here = feat // HEAD_DIM
    cubes_here = tok_rows // CUBE
    n_sel = pattern.shape[1]
    n_seq = lax.psum(1, "seq")
    me = lax.axis_index("seq")
    n_cubes = cubes_here * n_seq

    k3 = key_tokens.reshape(cubes_here, CUBE, feat)
    v3 = value_tokens.reshape(cubes_here, CUBE, feat)
    local_k = jnp.mean(k3.astype(jnp.float32), axis=1).astype(jnp.bfloat16)
    local_v = jnp.mean(v3.astype(jnp.float32), axis=1).astype(jnp.bfloat16)

    listed_me = jnp.any(
        pattern.reshape(-1)[:, None] == jnp.arange(n_cubes, dtype=jnp.int32)[None, :], axis=0
    ).astype(jnp.int32).reshape(n_seq, cubes_here)
    need_by = lax.all_to_all(listed_me, "seq", 0, 0, tiled=True) > 0
    pos_by = jnp.cumsum(need_by.astype(jnp.int32), axis=1) - 1
    hit = need_by[:, :, None] & (pos_by[:, :, None] == jnp.arange(CAP, dtype=jnp.int32)[None, None, :])
    send_idx = jnp.sum(jnp.where(hit, jnp.arange(cubes_here, dtype=jnp.int32)[None, :, None], 0), axis=1)

    kv_rows = CAP * CUBE
    okv = jnp.concatenate([k3, v3], axis=2)
    pooled = jnp.concatenate([local_k, local_v], axis=1)
    send = pl.pallas_call(
        pack_kernel,
        out_shape=jax.ShapeDtypeStruct((n_seq, kv_rows + cubes_here, 2 * feat), jnp.bfloat16),
        grid_spec=pltpu.PrefetchScalarGridSpec(
            num_scalar_prefetch=1,
            grid=(n_seq,),
            in_specs=[
                pl.BlockSpec((cubes_here, CUBE, 2 * feat), lambda b, t: (0, 0, 0)),
                pl.BlockSpec((cubes_here, 2 * feat), lambda b, t: (0, 0)),
            ],
            out_specs=pl.BlockSpec((None, kv_rows + cubes_here, 2 * feat), lambda b, t: (b, 0, 0)),
        ),
    )(send_idx, okv, pooled)
    recv = lax.all_to_all(send, "seq", 0, 0, tiled=True)

    pooled_k = recv[:, kv_rows:, :feat].reshape(n_cubes, feat)
    pooled_v = recv[:, kv_rows:, feat:].reshape(n_cubes, feat)

    rank_from = jnp.clip(jnp.cumsum(listed_me, axis=1) - 1, 0, CAP - 1)
    src = pattern // cubes_here
    loc = pattern % cubes_here
    own = src == me
    src_tbl = jnp.where(own, -1, src).astype(jnp.int32)
    row_tbl = jnp.where(own, loc, rank_from[src, loc] * CUBE).astype(jnp.int32)

    per_step = 2
    kern = functools.partial(attend_kernel, n_sel=n_sel, heads_here=heads_here, per_step=per_step)
    full2 = lambda i, a, r: (0, 0)
    hbm = pl.BlockSpec(memory_space=pl.ANY)
    attended = pl.pallas_call(
        kern,
        out_shape=jax.ShapeDtypeStruct((tok_rows, feat), jnp.bfloat16),
        grid_spec=pltpu.PrefetchScalarGridSpec(
            num_scalar_prefetch=2,
            grid=(cubes_here // per_step,),
            in_specs=[
                pl.BlockSpec((per_step * CUBE, feat), lambda i, a, r: (i, 0)),
                hbm,
                hbm,
                pl.BlockSpec((n_cubes, feat), full2),
                pl.BlockSpec((n_cubes, feat), full2),
            ],
            out_specs=pl.BlockSpec((per_step * CUBE, feat), lambda i, a, r: (i, 0)),
            scratch_shapes=[
                pltpu.VMEM((2, per_step, n_sel, CUBE, 2 * feat), jnp.bfloat16),
                pltpu.SemaphoreType.DMA((2,)),
            ],
        ),
        compiler_params=pltpu.CompilerParams(
            dimension_semantics=("arbitrary",), vmem_limit_bytes=32 * 1024 * 1024),
    )(src_tbl, row_tbl, queries, okv, recv, pooled_k, pooled_v)

    pair = ("yh", "core")
    n_pair = lax.psum(1, pair)
    n_x = lax.psum(1, "x")
    w_all = lax.all_gather(w_out, pair, axis=0, tiled=True)
    per_dest = attended.reshape(-1, n_x, 2, CUBE, feat)
    per_dest = jnp.transpose(per_dest, (0, 2, 1, 3, 4)).reshape(n_pair, n_x * CUBE, feat)
    me_pair = lax.axis_index(pair)
    partial = None
    for k in range(n_pair):
        if k == 0:
            got = lax.dynamic_index_in_dim(per_dest, me_pair, axis=0, keepdims=False)
        else:
            out = lax.dynamic_index_in_dim(per_dest, me_pair ^ k, axis=0, keepdims=False)
            got = lax.ppermute(out, pair, [(g, g ^ k) for g in range(n_pair)])
        rows = lax.dynamic_slice_in_dim(w_all, (me_pair ^ k) * feat, feat, axis=0)
        term = jnp.dot(got, rows, preferred_element_type=jnp.float32)
        term = term.astype(jnp.bfloat16).astype(jnp.float32)
        partial = term if partial is None else partial + term
    blocks = partial.astype(jnp.bfloat16).reshape(n_x, CUBE, -1)
    me_x = lax.axis_index("x")
    summed = lax.dynamic_index_in_dim(blocks, me_x, axis=0, keepdims=False).astype(jnp.float32)
    pick = lambda k: lax.dynamic_index_in_dim(blocks, (me_x + k) % n_x, axis=0, keepdims=False)
    if n_x == 4:
        up = [(g, (g + 1) % n_x) for g in range(n_x)]
        down = [(g, (g - 1) % n_x) for g in range(n_x)]
        half = CUBE // 2
        far = pick(2)
        got_up = lax.ppermute(jnp.concatenate([pick(1), far[:half]], axis=0), "x", up)
        got_down = lax.ppermute(jnp.concatenate([pick(3), far[half:]], axis=0), "x", down)
        relay_up = lax.ppermute(got_up[CUBE:], "x", up)
        relay_down = lax.ppermute(got_down[CUBE:], "x", down)
        summed = summed + got_up[:CUBE].astype(jnp.float32) + got_down[:CUBE].astype(jnp.float32)
        summed = summed + jnp.concatenate([relay_up, relay_down], axis=0).astype(jnp.float32)
    else:
        for k in range(1, n_x):
            got = lax.ppermute(pick(k), "x", [(g, (g + k) % n_x) for g in range(n_x)])
            summed = summed + got.astype(jnp.float32)
    return (summed * out_gate[None, :]).astype(jnp.bfloat16)


def solution(mesh):
    n_seq, n_head = mesh.devices.shape
    split = Mesh(mesh.devices.reshape(n_seq, 2, n_head // 4, 2), ("seq", "yh", "x", "core"))
    head = ("yh", "x", "core")
    return jax.shard_map(
        on_device,
        mesh=split,
        in_specs=(
            P("seq", head),
            P("seq", head),
            P("seq", head),
            P("seq", None),
            P(head, None),
            P(),
        ),
        out_specs=P(("seq", "yh", "x", "core"), None),
        check_vma=False,
    )
```

```python
import functools

import jax
import jax.numpy as jnp
from jax import lax
from jax.experimental import pallas as pl
from jax.experimental.pallas import tpu as pltpu
from jax.sharding import Mesh, PartitionSpec as P

HEAD_DIM = 128
CUBE = 64
CAP = 6


def attend_kernel(src_ref, row_ref, q_ref, okv_hbm, rv_hbm, pk_ref, pv_ref, o_ref,
                  kvbuf, sem, *, n_sel, heads_here, per_step):
    i = pl.program_id(0)
    steps = pl.num_programs(0)
    scale = HEAD_DIM ** (-0.5)

    def start(step, slot):
        for u in range(per_step):
            for j in range(n_sel):
                a = src_ref[step * per_step + u, j]
                r = row_ref[step * per_step + u, j]

                @pl.when(a < 0)
                def _():
                    pltpu.make_async_copy(okv_hbm.at[r], kvbuf.at[slot, u, j], sem.at[slot]).start()

                @pl.when(a >= 0)
                def _():
                    base = pl.multiple_of(r, CUBE)
                    pltpu.make_async_copy(
                        rv_hbm.at[a, pl.ds(base, CUBE)], kvbuf.at[slot, u, j], sem.at[slot]).start()

    @pl.when(i == 0)
    def _():
        start(0, 0)

    slot = i % 2

    @pl.when(i + 1 < steps)
    def _():
        start(i + 1, 1 - slot)

    pltpu.make_async_copy(kvbuf.at[slot], kvbuf.at[slot], sem.at[slot]).wait()

    def softmax_w(s):
        m = jnp.max(s, axis=-1, keepdims=True)
        p = jnp.exp(s - m)
        return (p / jnp.sum(p, axis=-1, keepdims=True)).astype(jnp.bfloat16)

    dims = (((1,), (1,)), ((), ()))
    for u in range(per_step):
        rows = pl.ds(u * CUBE, CUBE)
        for h in range(heads_here):
            cols = pl.ds(h * HEAD_DIM, HEAD_DIM)
            q = q_ref[rows, cols]
            k = kvbuf[slot, u, :, :, cols].reshape(n_sel * CUBE, HEAD_DIM)
            v = kvbuf[slot, u, :, :, pl.ds(heads_here * HEAD_DIM + h * HEAD_DIM, HEAD_DIM)].reshape(
                n_sel * CUBE, HEAD_DIM)
            s_f = lax.dot_general(q, k, dims, preferred_element_type=jnp.float32) * scale
            fine = jnp.dot(softmax_w(s_f), v, preferred_element_type=jnp.float32)
            s_c = lax.dot_general(q, pk_ref[:, cols], dims, preferred_element_type=jnp.float32) * scale
            coarse = jnp.dot(softmax_w(s_c), pv_ref[:, cols], preferred_element_type=jnp.float32)
            o_ref[rows, cols] = (fine + coarse).astype(jnp.bfloat16)


def pack_kernel(idx_ref, kv_ref, pooled_ref, o_ref):
    per = o_ref.shape[0]
    for d in range(per):
        b = pl.program_id(0) * per + d
        for r in range(CAP):
            o_ref[d, pl.ds(r * CUBE, CUBE), :] = kv_ref[idx_ref[b, r]]
        o_ref[d, pl.ds(CAP * CUBE, pooled_ref.shape[0]), :] = pooled_ref[...]


def on_device(queries, key_tokens, value_tokens, pattern, w_out, out_gate):
    tok_rows, feat = queries.shape
    heads_here = feat // HEAD_DIM
    cubes_here = tok_rows // CUBE
    n_sel = pattern.shape[1]
    n_seq = lax.psum(1, "seq")
    me = lax.axis_index("seq")
    n_cubes = cubes_here * n_seq

    k3 = key_tokens.reshape(cubes_here, CUBE, feat)
    v3 = value_tokens.reshape(cubes_here, CUBE, feat)
    local_k = jnp.mean(k3.astype(jnp.float32), axis=1).astype(jnp.bfloat16)
    local_v = jnp.mean(v3.astype(jnp.float32), axis=1).astype(jnp.bfloat16)

    listed_me = jnp.any(
        pattern.reshape(-1)[:, None] == jnp.arange(n_cubes, dtype=jnp.int32)[None, :], axis=0
    ).astype(jnp.int32).reshape(n_seq, cubes_here)
    need_by = lax.all_to_all(listed_me, "seq", 0, 0, tiled=True) > 0
    pos_by = jnp.cumsum(need_by.astype(jnp.int32), axis=1) - 1
    hit = need_by[:, :, None] & (pos_by[:, :, None] == jnp.arange(CAP, dtype=jnp.int32)[None, None, :])
    send_idx = jnp.sum(jnp.where(hit, jnp.arange(cubes_here, dtype=jnp.int32)[None, :, None], 0), axis=1)

    kv_rows = CAP * CUBE
    okv = jnp.concatenate([k3, v3], axis=2)
    pooled = jnp.concatenate([local_k, local_v], axis=1)
    send = pl.pallas_call(
        pack_kernel,
        out_shape=jax.ShapeDtypeStruct((n_seq, kv_rows + cubes_here, 2 * feat), jnp.bfloat16),
        grid_spec=pltpu.PrefetchScalarGridSpec(
            num_scalar_prefetch=1,
            grid=(n_seq // 2,),
            in_specs=[
                pl.BlockSpec((cubes_here, CUBE, 2 * feat), lambda b, t: (0, 0, 0)),
                pl.BlockSpec((cubes_here, 2 * feat), lambda b, t: (0, 0)),
            ],
            out_specs=pl.BlockSpec((2, kv_rows + cubes_here, 2 * feat), lambda b, t: (b, 0, 0)),
        ),
    )(send_idx, okv, pooled)
    recv = lax.all_to_all(send, "seq", 0, 0, tiled=True)

    pooled_k = recv[:, kv_rows:, :feat].reshape(n_cubes, feat)
    pooled_v = recv[:, kv_rows:, feat:].reshape(n_cubes, feat)

    rank_from = jnp.clip(jnp.cumsum(listed_me, axis=1) - 1, 0, CAP - 1)
    src = pattern // cubes_here
    loc = pattern % cubes_here
    own = src == me
    src_tbl = jnp.where(own, -1, src).astype(jnp.int32)
    row_tbl = jnp.where(own, loc, rank_from[src, loc] * CUBE).astype(jnp.int32)

    per_step = 2
    kern = functools.partial(attend_kernel, n_sel=n_sel, heads_here=heads_here, per_step=per_step)
    full2 = lambda i, a, r: (0, 0)
    hbm = pl.BlockSpec(memory_space=pl.ANY)
    attended = pl.pallas_call(
        kern,
        out_shape=jax.ShapeDtypeStruct((tok_rows, feat), jnp.bfloat16),
        grid_spec=pltpu.PrefetchScalarGridSpec(
            num_scalar_prefetch=2,
            grid=(cubes_here // per_step,),
            in_specs=[
                pl.BlockSpec((per_step * CUBE, feat), lambda i, a, r: (i, 0)),
                hbm,
                hbm,
                pl.BlockSpec((n_cubes, feat), full2),
                pl.BlockSpec((n_cubes, feat), full2),
            ],
            out_specs=pl.BlockSpec((per_step * CUBE, feat), lambda i, a, r: (i, 0)),
            scratch_shapes=[
                pltpu.VMEM((2, per_step, n_sel, CUBE, 2 * feat), jnp.bfloat16),
                pltpu.SemaphoreType.DMA((2,)),
            ],
        ),
        compiler_params=pltpu.CompilerParams(
            dimension_semantics=("arbitrary",), vmem_limit_bytes=32 * 1024 * 1024),
    )(src_tbl, row_tbl, queries, okv, recv, pooled_k, pooled_v)

    pair = ("yh", "core")
    n_pair = lax.psum(1, pair)
    n_x = lax.psum(1, "x")
    w_all = lax.all_gather(w_out, pair, axis=0, tiled=True)
    per_dest = attended.reshape(-1, n_x, 2, CUBE, feat)
    per_dest = jnp.transpose(per_dest, (0, 2, 1, 3, 4)).reshape(n_pair, n_x * CUBE, feat)
    me_pair = lax.axis_index(pair)
    partial = None
    for k in range(n_pair):
        if k == 0:
            got = lax.dynamic_index_in_dim(per_dest, me_pair, axis=0, keepdims=False)
        else:
            out = lax.dynamic_index_in_dim(per_dest, me_pair ^ k, axis=0, keepdims=False)
            got = lax.ppermute(out, pair, [(g, g ^ k) for g in range(n_pair)])
        rows = lax.dynamic_slice_in_dim(w_all, (me_pair ^ k) * feat, feat, axis=0)
        term = jnp.dot(got, rows, preferred_element_type=jnp.float32)
        term = term.astype(jnp.bfloat16).astype(jnp.float32)
        partial = term if partial is None else partial + term
    blocks = partial.astype(jnp.bfloat16).reshape(n_x, CUBE, -1)
    me_x = lax.axis_index("x")
    summed = lax.dynamic_index_in_dim(blocks, me_x, axis=0, keepdims=False).astype(jnp.float32)
    for k in range(1, n_x):
        out = lax.dynamic_index_in_dim(blocks, (me_x + k) % n_x, axis=0, keepdims=False)
        got = lax.ppermute(out, "x", [(g, (g + k) % n_x) for g in range(n_x)])
        summed = summed + got.astype(jnp.float32)
    return (summed * out_gate[None, :]).astype(jnp.bfloat16)


def solution(mesh):
    n_seq, n_head = mesh.devices.shape
    split = Mesh(mesh.devices.reshape(n_seq, 2, n_head // 4, 2), ("seq", "yh", "x", "core"))
    head = ("yh", "x", "core")
    return jax.shard_map(
        on_device,
        mesh=split,
        in_specs=(
            P("seq", head),
            P("seq", head),
            P("seq", head),
            P("seq", None),
            P(head, None),
            P(),
        ),
        out_specs=P(("seq", "yh", "x", "core"), None),
        check_vma=False,
    )
```
